256 devices in a mesh: req: 32 (over z_hi, x, y), cand: 8 (over z_lo, core).
Axes of the slice: x: 4, y: 4, z: 8 (z_hi: 2, z_lo: 4; z = z_hi * 4 + z_lo), core: 2. Of those that a mesh axis runs over, the one named last changes fastest.
Arguments:
- item_table: bfloat16 [32, 8, 256, 1024], P('req', 'cand'), may hold values from -25 to 25
- picked_items: int32 [32, 8, 1024], P('req', 'cand'), may hold values from 0 to 255
- destination: int32 [32, 8, 1024], P('req', 'cand'), may hold values from 0 to 31, as said below
- slot_index: int32 [32, 8, 1024], P('req', 'cand'), may hold values from 0 to 1023, as said below
- history_cache: bfloat16 [32, 8, 128, 2048], P('req', 'cand'), may hold values from -6 to 6
- history_length: int32 [32, 8], P('req'), may hold values from 16 to 128
- input_weight: bfloat16 [1024, 4096], replicated, may hold values from -0.1875 to 0.1875
- output_weight: bfloat16 [1024, 1024], replicated, may hold values from -0.1875 to 0.1875
Outputs:
- cand_out: bfloat16 [32, 8, 1024, 1024], P('req', 'cand')
The draws below stay inside these ranges and needn't reach their ends.
Inputs may be any that keep to these rules, and one draw needn't show every extreme that they name: Each device sends exactly 1024 rows, and within each index of cand every device receives exactly 1024; no device sends more than 64 rows to one destination, and within each index of cand some device sends exactly 64 to one destination. `slot_index`: the rows that reach one device fill each of its 1024 slots exactly once.
All inputs are finite; a program needn't handle non-finite values.
Results may differ from the reference program's by a relative error of at most 0.005.
Values may be sent and summed in bfloat16 or wider, within the bound.
No kernel may reach another device: no remote copies, remote signals or barrier semaphores. Data moves between devices by JAX's collectives and lax.ppermute only.
A program may use at most 128 MiB of HBM per device.

```python
import math
import jax
import jax.numpy as jnp
from jax import lax

D = 1024
HEADS = 8
HIST = 128
TAB = 256
CAND_DEV = 1024
N_REQ = 32
N_CAND = 8


def draw_item_table(key, part):
    subkeys = jax.random.split(jax.random.fold_in(key, 3), 3)
    full_shape = (N_REQ, N_CAND, TAB, D)
    samples = jnp.clip(jax.random.normal(subkeys[0], full_shape, jnp.float32), -4.0, 4.0)
    row_scale = jnp.exp(jax.random.uniform(subkeys[1], (N_REQ, N_CAND, TAB, 1), jnp.float32, 0.0, math.log(10.0)))
    column_scale = jnp.exp(jax.random.uniform(subkeys[2], (1, 1, 1, D), jnp.float32, 0.0, math.log(10.0)))
    return (samples * row_scale * column_scale / 16.0).astype(jnp.bfloat16)


def column_plan(column_key):
    subkeys = jax.random.split(column_key, 4)
    average_load = CAND_DEV // N_REQ
    half_count = N_REQ // 2
    offsets = jax.random.permutation(subkeys[0], N_REQ).astype(jnp.int32)
    offset_shift = jax.random.randint(subkeys[1], (half_count,), 0, average_load + 1).astype(jnp.int32)
    offset_shift = offset_shift.at[0].set(average_load)
    loads = jnp.stack([average_load + offset_shift, average_load - offset_shift], axis=1).reshape(N_REQ)
    ends = jnp.cumsum(loads).astype(jnp.int32)
    begins = ends - loads
    entries = jnp.arange(CAND_DEV, dtype=jnp.int32)
    bucket = jnp.sum((entries[:, None] >= ends[None, :]).astype(jnp.int32), axis=1)
    within = entries - begins[bucket]
    sources = jnp.arange(N_REQ, dtype=jnp.int32)
    targets = (sources[:, None] + offsets[bucket][None, :]) % N_REQ
    inverse = jnp.zeros(N_REQ, jnp.int32).at[offsets].set(sources)
    counts = loads[inverse[(sources[None, :] - sources[:, None]) % N_REQ]]
    starting = (jnp.cumsum(counts, axis=0) - counts).astype(jnp.int32)
    receive_order = jax.vmap(lambda sub_key: jax.random.permutation(sub_key, CAND_DEV))(jax.random.split(subkeys[2], N_REQ)).astype(jnp.int32)
    arrival = starting[sources[:, None], targets] + within[None, :]
    places = receive_order[targets, arrival]
    send_order = jax.vmap(lambda sub_key: jax.random.permutation(sub_key, CAND_DEV))(jax.random.split(subkeys[3], N_REQ)).astype(jnp.int32)
    dest_list = jnp.zeros((N_REQ, CAND_DEV), jnp.int32).at[sources[:, None], send_order].set(targets)
    slot_list = jnp.zeros((N_REQ, CAND_DEV), jnp.int32).at[sources[:, None], send_order].set(places)
    return (dest_list, slot_list)


def delivery_plan(key):
    column_keys = jax.random.split(jax.random.fold_in(key, 7), N_CAND)
    dest_all, slot_all = jax.vmap(column_plan)(column_keys)
    return (jnp.transpose(dest_all, (1, 0, 2)), jnp.transpose(slot_all, (1, 0, 2)))


def draw_destination(key, part):
    return delivery_plan(key)[0]


def draw_slot_index(key, part):
    return delivery_plan(key)[1]


def draw_history_length(key, part):
    subkeys = jax.random.split(jax.random.fold_in(key, 11), 3)
    total_count = N_REQ * N_CAND
    values = jax.random.randint(subkeys[0], (total_count,), HIST // 8, HIST + 1).astype(jnp.int32)
    longest = jax.random.randint(subkeys[1], (), 0, total_count)
    shortest = (longest + 1 + jax.random.randint(subkeys[2], (), 0, total_count - 1)) % total_count
    values = values.at[longest].set(HIST).at[shortest].set(HIST // 8)
    return values.reshape(N_REQ, N_CAND)


def place_ends(drawn, key, low, high):
    spot = [jax.random.randint(jax.random.fold_in(key, axis), (), 0, length) for axis, length in enumerate(drawn.shape)]
    widest = drawn.shape.index(max(drawn.shape))
    neighbour = spot[:widest] + [(spot[widest] + 1) % drawn.shape[widest]] + spot[widest + 1:]
    return drawn.at[tuple(spot)].set(low).at[tuple(neighbour)].set(high)


def block_levels(key, extent, cuts, low, largest):
    gain, own = 1.0, jax.random.fold_in(key, 6)
    for position, shards_of in cuts:
        heights = jnp.exp(jax.random.uniform(jax.random.fold_in(own, position), (shards_of,), jnp.float32, low / len(cuts), largest / len(cuts)))
        gain = gain * jnp.repeat(heights, extent[position] // shards_of).reshape([-1 if axis == position else 1 for axis in range(len(extent))])
    return gain


def gaussian(own_key, shape, deviation, most, shards=(), kind=jnp.bfloat16):
    values = deviation * jax.random.normal(own_key, shape, jnp.float32)
    if shards:
        values = values * block_levels(own_key, shape, shards, -0.22, 0.18)
    return jnp.clip(values, -most, most).astype(kind)


def setup_inputs(seed: int = 0) -> dict:
    splits = jax.random.split(jax.random.key(seed), 9)
    return {
        "item_table": draw_item_table(jax.random.fold_in(splits[8], 71), 0),
        "picked_items": place_ends(jax.random.randint(splits[1], (N_REQ, N_CAND, CAND_DEV), 0, TAB), jax.random.fold_in(splits[1], 1), 0, TAB - 1).astype(jnp.int32),
        "destination": draw_destination(jax.random.fold_in(splits[8], 71), 0),
        "slot_index": draw_slot_index(jax.random.fold_in(splits[8], 71), 0),
        "history_cache": gaussian(splits[4], (N_REQ, N_CAND, HIST, 2 * D), 1.0, 6.0, ((0, 32), (1, 8))),
        "history_length": draw_history_length(jax.random.fold_in(splits[8], 71), 0),
        "input_weight": gaussian(splits[6], (D, 4 * D), D ** -0.5, 0.1875),
        "output_weight": gaussian(splits[7], (D, D), D ** -0.5, 0.1875),
    }


epsilon = 1e-06

def layer_norm(values):
    average = lax.optimization_barrier(jnp.mean(values, axis=-1, keepdims=True))
    centred = values - average
    variance = lax.optimization_barrier(jnp.mean(centred * centred, axis=-1, keepdims=True))
    return centred * lax.rsqrt(variance + epsilon)

def take_rows(rows_in, chosen):
    return jnp.take(rows_in, chosen, axis=0)

def reference(item_table, picked_items, destination, slot_index, history_cache, history_length, input_weight, output_weight):
    sources, members, slot_count = picked_items.shape
    feature = item_table.shape[-1]
    picked = jax.vmap(jax.vmap(take_rows))(item_table, picked_items)
    column = jnp.broadcast_to(jnp.arange(members, dtype=jnp.int32)[None, :, None], destination.shape)
    arranged = jnp.zeros((sources, members, slot_count, feature), jnp.bfloat16).at[destination, column, slot_index].set(picked)
    per_request = slot_count // members
    head_width = feature // HEADS
    score_scale = 1.0 / math.sqrt(head_width)

    def one_group(operands):
        group_rows, group_cache, lengths = operands
        as_float = group_rows.astype(jnp.float32)
        normed_in = layer_norm(as_float).astype(jnp.bfloat16)
        projected = jax.nn.silu(jnp.dot(normed_in.reshape(-1, feature), input_weight, preferred_element_type=jnp.float32)).astype(jnp.bfloat16)
        quarters = projected.reshape(members, members, per_request, 4, HEADS, head_width).astype(jnp.float32)
        gate_u = quarters[:, :, :, 0]
        own_values = quarters[:, :, :, 1]
        queries = quarters[:, :, :, 2]
        own_keys = quarters[:, :, :, 3]
        keys = group_cache[:, :, :feature].reshape(members, HIST, HEADS, head_width).astype(jnp.float32)
        values = group_cache[:, :, feature:].reshape(members, HIST, HEADS, head_width).astype(jnp.float32)
        length_plus = lengths.astype(jnp.float32) + 1.0
        scores = jnp.einsum('cbihe,bjhe->cbhij', queries, keys) * score_scale
        valid = (jnp.arange(HIST, dtype=jnp.int32)[None, :] < lengths[:, None]).astype(jnp.float32)
        weights = (jax.nn.silu(scores) / length_plus[None, :, None, None, None] * valid[None, :, None, None, :]).astype(jnp.bfloat16)
        history_part = jnp.einsum('cbhij,bjhe->cbihe', weights.astype(jnp.float32), values)
        own_scores = lax.optimization_barrier(jnp.sum(queries * own_keys, axis=-1)) * score_scale
        own_term = (jax.nn.silu(own_scores) / length_plus[None, :, None, None])[..., None] * own_values
        attended = (history_part + own_term).reshape(members, slot_count, feature)
        normed_out = layer_norm(attended)
        gated = (normed_out * gate_u.reshape(members, slot_count, feature)).astype(jnp.bfloat16)
        update = jnp.dot(gated.reshape(-1, feature), output_weight, preferred_element_type=jnp.float32)
        mixed = as_float + update.reshape(members, slot_count, feature)
        return mixed.astype(jnp.bfloat16)
    return lax.map(one_group, (arranged, history_cache, history_length))
```

```python
import math

import jax
import jax.numpy as jnp
from jax import lax
from jax.sharding import Mesh
from jax.sharding import PartitionSpec as P

HEADS = 8
HALVES = 2


epsilon = 1e-06


def layer_norm(values):
    average = jnp.mean(values, axis=-1, keepdims=True)
    centred = values - average
    variance = jnp.mean(centred * centred, axis=-1, keepdims=True)
    return centred * lax.rsqrt(variance + epsilon)


def attend(queries, cache_rows, lengths, head_count, score_scale):
    count_req, history_span, doubled = cache_rows.shape
    feature = doubled // 2
    head_width = feature // head_count
    keys = cache_rows[:, :, :feature].reshape(count_req, history_span, head_count, head_width)
    values = cache_rows[:, :, feature:].reshape(count_req, history_span, head_count, head_width)
    scores = (
        jnp.einsum("bihe,bjhe->bhij", queries, keys, preferred_element_type=jnp.float32)
        * score_scale
    )
    positions = jnp.arange(history_span, dtype=jnp.int32)
    valid = (positions[None, :] < lengths[:, None]).astype(jnp.float32)
    length_plus = lengths.astype(jnp.float32) + 1.0
    weights = (
        jax.nn.silu(scores) / length_plus[:, None, None, None] * valid[:, None, None, :]
    ).astype(jnp.bfloat16)
    return jnp.einsum("bhij,bjhe->bihe", weights, values, preferred_element_type=jnp.float32)


def ranks(targets, sources):
    count = targets.shape[0]
    one_hot = (targets[:, None] == jnp.arange(sources, dtype=jnp.int32)[None, :])
    rows = jnp.arange(count, dtype=jnp.int32)
    lower = (rows[None, :] < rows[:, None]).astype(jnp.bfloat16)
    earlier = jnp.dot(lower, one_hot.astype(jnp.bfloat16), preferred_element_type=jnp.float32)
    return jnp.sum(jnp.where(one_hot, earlier, 0.0), axis=1).astype(jnp.int32)


def block_plan(ints, half, n_half, per_pair, sources):
    picks, targets, places = ints[0], ints[1], ints[2]
    within = ranks(targets, sources)
    keep = (targets // n_half) == half
    position = jnp.where(keep, (targets % n_half) * per_pair + within, -1)
    spots = jnp.arange(n_half * per_pair, dtype=jnp.int32)
    hit = position[None, :] == spots[:, None]
    row = jnp.sum(jnp.where(hit, picks[None, :], 0), axis=1)
    slot = jnp.sum(jnp.where(hit, places[None, :] + 1, 0), axis=1) - 1
    return row.reshape(n_half, per_pair), slot.reshape(n_half, per_pair)


def shards(
    item_table,
    picked_items,
    destination,
    slot_index,
    history_cache,
    history_length,
    input_weight,
    output_weight,
):
    n_half = lax.axis_size("xy")
    sources = HALVES * n_half
    half = lax.axis_index("zh")
    item_rows = item_table[0, 0]
    ints = jnp.stack([picked_items[0, 0], destination[0, 0], slot_index[0, 0]])
    slot_count = ints.shape[1]
    feature = item_rows.shape[1]
    per_pair = 2 * slot_count // sources
    swap = [(0, 1), (1, 0)]
    other_rows = lax.ppermute(item_rows, "zh", swap)
    other_ints = lax.ppermute(ints, "zh", swap)

    own_row, own_slot = block_plan(ints, half, n_half, per_pair, sources)
    far_row, far_slot = block_plan(other_ints, half, n_half, per_pair, sources)
    own_data = jnp.take(item_rows, own_row.reshape(-1), axis=0).reshape(n_half, per_pair, feature)
    far_data = jnp.take(other_rows, far_row.reshape(-1), axis=0).reshape(n_half, per_pair, feature)
    slots = jnp.concatenate([own_slot, far_slot], axis=1)
    capacity = 2 * per_pair
    radix = 32
    high = jnp.floor_divide(slots, radix)
    low = slots - high * radix
    tag_row = jnp.zeros((n_half, 8, feature), jnp.float32)
    tag_row = tag_row.at[:, 0, :capacity].set(high.astype(jnp.float32))
    tag_row = tag_row.at[:, 0, capacity : 2 * capacity].set(low.astype(jnp.float32))
    outgoing = jnp.concatenate(
        [own_data, far_data, tag_row.astype(jnp.bfloat16)], axis=1
    )
    arrived = lax.all_to_all(outgoing, "xy", split_axis=0, concat_axis=0, tiled=True)
    arrived_rows = arrived[:, :capacity].reshape(n_half * capacity, feature)
    tags = (
        arrived[:, capacity, :capacity].astype(jnp.int32) * radix
        + arrived[:, capacity, capacity : 2 * capacity].astype(jnp.int32)
    ).reshape(-1)
    slot_ids = jnp.arange(slot_count, dtype=jnp.int32)
    order = jnp.arange(n_half * capacity, dtype=jnp.int32)
    fill = jnp.sum(jnp.where(tags[None, :] == slot_ids[:, None], order[None, :], 0), axis=1)
    arranged = jnp.take(arrived_rows, fill, axis=0)

    lengths = history_length[0]
    members = lengths.shape[0]
    per_request = slot_count // members
    head_count = HEADS
    head_width = feature // head_count
    score_scale = 1.0 / math.sqrt(head_width)
    as_float = arranged.astype(jnp.float32)
    normed_in = layer_norm(as_float).astype(jnp.bfloat16)
    projected = jax.nn.silu(
        jnp.dot(normed_in, input_weight, preferred_element_type=jnp.float32)
    ).astype(jnp.bfloat16)
    quarters = projected.reshape(members, per_request, 4, head_count, head_width)
    gate_u = projected[:, :feature]
    own_values = quarters[:, :, 1]
    queries = quarters[:, :, 2]
    own_keys = quarters[:, :, 3]
    length_plus = lengths.astype(jnp.float32) + 1.0
    own_scores = (
        jnp.einsum("bihe,bihe->bih", queries, own_keys, preferred_element_type=jnp.float32)
        * score_scale
    )
    own_weight = jax.nn.silu(own_scores) / length_plus[:, None, None]
    own_term = own_weight[..., None] * own_values.astype(jnp.float32)
    found = attend(
        queries,
        lax.all_gather(history_cache, "cand", axis=1, tiled=True)[0],
        lengths,
        head_count,
        score_scale,
    )
    attended = (found + own_term).reshape(slot_count, feature)
    normed_out = layer_norm(attended)
    gated = (normed_out * gate_u.astype(jnp.float32)).astype(jnp.bfloat16)
    mixed = as_float + jnp.dot(gated, output_weight, preferred_element_type=jnp.float32)
    return mixed.astype(jnp.bfloat16)[None, None]


def solution(mesh):
    n_req, n_cand = mesh.devices.shape
    devices = mesh.devices.reshape(HALVES, n_req // HALVES, n_cand)
    split = Mesh(devices, ("zh", "xy", "cand"))
    req = ("zh", "xy")
    in_specs = (
        P(req, "cand", None, None),
        P(req, "cand", None),
        P(req, "cand", None),
        P(req, "cand", None),
        P(req, "cand", None, None),
        P(req, None),
        P(),
        P(),
    )
    out_specs = P(req, "cand", None, None)
    return jax.shard_map(shards, mesh=split, in_specs=in_specs, out_specs=out_specs, check_vma=False)
```

```python
import math

import jax
import jax.numpy as jnp
from jax import lax
from jax.sharding import Mesh
from jax.sharding import PartitionSpec as P

HEADS = 8
HALVES = 2


epsilon = 1e-06


def layer_norm(values):
    average = jnp.mean(values, axis=-1, keepdims=True)
    centred = values - average
    variance = jnp.mean(centred * centred, axis=-1, keepdims=True)
    return centred * lax.rsqrt(variance + epsilon)


def ranks(targets, sources):
    count = targets.shape[0]
    one_hot = (targets[:, None] == jnp.arange(sources, dtype=jnp.int32)[None, :])
    rows = jnp.arange(count, dtype=jnp.int32)
    lower = (rows[None, :] < rows[:, None]).astype(jnp.bfloat16)
    earlier = jnp.dot(lower, one_hot.astype(jnp.bfloat16), preferred_element_type=jnp.float32)
    return jnp.sum(jnp.where(one_hot, earlier, 0.0), axis=1).astype(jnp.int32)


def block_plan(ints, half, n_half, per_pair, sources):
    picks, targets, places = ints[0], ints[1], ints[2]
    within = ranks(targets, sources)
    keep = (targets // n_half) == half
    position = jnp.where(keep, (targets % n_half) * per_pair + within, -1)
    spots = jnp.arange(n_half * per_pair, dtype=jnp.int32)
    hit = position[None, :] == spots[:, None]
    row = jnp.sum(jnp.where(hit, picks[None, :], 0), axis=1)
    slot = jnp.sum(jnp.where(hit, places[None, :] + 1, 0), axis=1) - 1
    return row.reshape(n_half, per_pair), slot.reshape(n_half, per_pair)


def select_rows(table, rows, slots):
    flat_rows = rows.reshape(-1)
    used = slots.reshape(-1) >= 0
    entries = jnp.arange(table.shape[0], dtype=jnp.int32)
    one_hot = ((flat_rows[:, None] == entries[None, :]) & used[:, None]).astype(table.dtype)
    picked = jnp.dot(one_hot, table, preferred_element_type=jnp.float32).astype(table.dtype)
    return picked.reshape(rows.shape + (table.shape[1],))


def shards(
    item_table,
    picked_items,
    destination,
    slot_index,
    history_cache,
    history_length,
    input_weight,
    output_weight,
):
    n_half = lax.axis_size("xy")
    sources = HALVES * n_half
    half = lax.axis_index("zh")
    item_rows = item_table[0, 0]
    ints = jnp.stack([picked_items[0, 0], destination[0, 0], slot_index[0, 0]])
    slot_count = ints.shape[1]
    feature = item_rows.shape[1]
    per_pair = 2 * slot_count // sources
    swap = [(0, 1), (1, 0)]
    other_rows = lax.ppermute(item_rows, "zh", swap)
    other_ints = lax.ppermute(ints, "zh", swap)

    own_row, own_slot = block_plan(ints, half, n_half, per_pair, sources)
    far_row, far_slot = block_plan(other_ints, half, n_half, per_pair, sources)
    own_data = select_rows(item_rows, own_row, own_slot)
    far_data = select_rows(other_rows, far_row, far_slot)
    slots = jnp.concatenate([own_slot, far_slot], axis=1)
    capacity = 2 * per_pair
    tag_rows = 16
    radix = 32
    high = jnp.floor_divide(slots, radix)
    low = slots - high * radix
    spare = jnp.zeros((n_half, feature - 2 * capacity), jnp.int32)
    tag_line = jnp.concatenate([high, low, spare], axis=1).astype(jnp.bfloat16)
    tag_block = jnp.concatenate(
        [tag_line[:, None, :], jnp.zeros((n_half, tag_rows - 1, feature), jnp.bfloat16)], axis=1
    )
    outgoing = jnp.concatenate([own_data, far_data, tag_block], axis=1)
    arrived = lax.all_to_all(outgoing, "xy", split_axis=0, concat_axis=0, tiled=True)
    block = capacity + tag_rows
    arrived_rows = arrived.reshape(n_half * block, feature)
    tags = (
        arrived[:, capacity, :capacity].astype(jnp.int32) * radix
        + arrived[:, capacity, capacity : 2 * capacity].astype(jnp.int32)
    ).reshape(-1)
    slot_ids = jnp.arange(slot_count, dtype=jnp.int32)
    order = jnp.arange(n_half * capacity, dtype=jnp.int32)
    order = (order // capacity) * block + order % capacity
    fill = jnp.sum(jnp.where(tags[None, :] == slot_ids[:, None], order[None, :], 0), axis=1)
    arranged = jnp.take(arrived_rows, fill, axis=0)

    lengths = history_length[0]
    members = lengths.shape[0]
    per_request = slot_count // members
    head_count = HEADS
    head_width = feature // head_count
    score_scale = 1.0 / math.sqrt(head_width)
    as_float = arranged.astype(jnp.float32)
    normed_in = layer_norm(as_float).astype(jnp.bfloat16)
    projected = jax.nn.silu(
        jnp.dot(normed_in, input_weight, preferred_element_type=jnp.float32)
    ).astype(jnp.bfloat16)
    gate_u = projected[:, :feature]
    length_plus = lengths.astype(jnp.float32) + 1.0
    cache = lax.all_gather(history_cache, "cand", axis=1, tiled=True)[0]
    history_span = cache.shape[1]
    positions = jnp.arange(history_span, dtype=jnp.int32)
    valid = (positions[None, :] < lengths[:, None]).astype(jnp.float32)
    outputs = []
    for head in range(head_count):
        def part(block, offset=head * head_width):
            start = block * feature + offset
            return projected[:, start : start + head_width].reshape(members, per_request, head_width)
        own_values, queries, own_keys = part(1), part(2), part(3)
        keys = cache[:, :, head * head_width : (head + 1) * head_width]
        values = cache[:, :, feature + head * head_width : feature + (head + 1) * head_width]
        scores = (
            jnp.einsum("bie,bje->bij", queries, keys, preferred_element_type=jnp.float32)
            * score_scale
        )
        weights = (
            jax.nn.silu(scores) / length_plus[:, None, None] * valid[:, None, :]
        ).astype(jnp.bfloat16)
        found = jnp.einsum("bij,bje->bie", weights, values, preferred_element_type=jnp.float32)
        own_scores = (
            jnp.sum(queries.astype(jnp.float32) * own_keys.astype(jnp.float32), axis=-1)
            * score_scale
        )
        own_weight = jax.nn.silu(own_scores) / length_plus[:, None]
        outputs.append(found + own_weight[..., None] * own_values.astype(jnp.float32))
    attended = jnp.concatenate(outputs, axis=-1).reshape(slot_count, feature)
    normed_out = layer_norm(attended)
    gated = (normed_out * gate_u.astype(jnp.float32)).astype(jnp.bfloat16)
    mixed = as_float + jnp.dot(gated, output_weight, preferred_element_type=jnp.float32)
    return mixed.astype(jnp.bfloat16)[None, None]


def solution(mesh):
    n_req, n_cand = mesh.devices.shape
    devices = mesh.devices.reshape(HALVES, n_req // HALVES, n_cand)
    split = Mesh(devices, ("zh", "xy", "cand"))
    req = ("zh", "xy")
    in_specs = (
        P(req, "cand", None, None),
        P(req, "cand", None),
        P(req, "cand", None),
        P(req, "cand", None),
        P(req, "cand", None, None),
        P(req, None),
        P(),
        P(),
    )
    out_specs = P(req, "cand", None, None)
    return jax.shard_map(shards, mesh=split, in_specs=in_specs, out_specs=out_specs, check_vma=False)
```

```python
import math

import functools

import jax
import jax.numpy as jnp
from jax import lax
from jax.experimental import pallas as pl
from jax.experimental.pallas import tpu as pltpu
from jax.sharding import Mesh
from jax.sharding import PartitionSpec as P

HEADS = 8
HALVES = 2


epsilon = 1e-06


def layer_norm(values):
    average = jnp.mean(values, axis=-1, keepdims=True)
    centred = values - average
    variance = jnp.mean(centred * centred, axis=-1, keepdims=True)
    return centred * lax.rsqrt(variance + epsilon)


def silu(v):
    return v / (1.0 + jnp.exp(-v))

def tail_kernel(len_ref, proj_ref, cache_ref, rows_ref, wout_ref, out_ref, att_ref, *, heads, eps):
    b = pl.program_id(0)
    feature = rows_ref.shape[1]
    head_width = feature // heads
    hist = cache_ref.shape[1]
    scale = 1.0 / math.sqrt(head_width)
    length = len_ref[b]
    length_plus = length.astype(jnp.float32) + 1.0
    valid = lax.broadcasted_iota(jnp.int32, (1, hist), 1) < length
    for h in range(heads):
        lo = h * head_width
        q = proj_ref[:, 2 * feature + lo : 2 * feature + lo + head_width]
        k = cache_ref[0, :, lo : lo + head_width]
        v = cache_ref[0, :, feature + lo : feature + lo + head_width]
        s = lax.dot_general(q, k, (((1,), (1,)), ((), ())), preferred_element_type=jnp.float32) * scale
        w = jnp.where(valid, silu(s) / length_plus, 0.0).astype(jnp.bfloat16)
        found = jnp.dot(w, v, preferred_element_type=jnp.float32)
        own_k = proj_ref[:, 3 * feature + lo : 3 * feature + lo + head_width].astype(jnp.float32)
        own_v = proj_ref[:, feature + lo : feature + lo + head_width].astype(jnp.float32)
        own_s = jnp.sum(q.astype(jnp.float32) * own_k, axis=-1, keepdims=True) * scale
        att_ref[:, lo : lo + head_width] = found + (silu(own_s) / length_plus) * own_v
    att = att_ref[...]
    mean = jnp.mean(att, axis=-1, keepdims=True)
    centred = att - mean
    var = jnp.mean(centred * centred, axis=-1, keepdims=True)
    normed = centred * lax.rsqrt(var + eps)
    gated = (normed * proj_ref[:, 0:feature].astype(jnp.float32)).astype(jnp.bfloat16)
    update = jnp.dot(gated, wout_ref[...], preferred_element_type=jnp.float32)
    out_ref[...] = (rows_ref[...].astype(jnp.float32) + update).astype(out_ref.dtype)

def tail(lengths, projected, cache, rows, wout, heads=8, eps=1e-6):
    members, hist, doubled = cache.shape
    slots, feature = rows.shape
    per = slots // members
    width = projected.shape[1]
    kern = functools.partial(tail_kernel, heads=heads, eps=eps)
    spec = pltpu.PrefetchScalarGridSpec(
        num_scalar_prefetch=1, grid=(members,),
        in_specs=[pl.BlockSpec((per, width), lambda b, n: (b, 0)),
                  pl.BlockSpec((1, hist, doubled), lambda b, n: (b, 0, 0)),
                  pl.BlockSpec((per, feature), lambda b, n: (b, 0)),
                  pl.BlockSpec((feature, feature), lambda b, n: (0, 0))],
        out_specs=pl.BlockSpec((per, feature), lambda b, n: (b, 0)),
        scratch_shapes=[pltpu.VMEM((per, feature), jnp.float32)])
    return pl.pallas_call(kern, grid_spec=spec, out_shape=jax.ShapeDtypeStruct((slots, feature), jnp.bfloat16),
        cost_estimate=pl.CostEstimate(flops=2*slots*feature*feature + 4*slots*hist*feature, transcendentals=slots*(hist*heads+heads), bytes_accessed=slots*width*2 + members*hist*doubled*2 + 2*slots*feature*2 + feature*feature*2))(lengths, projected, cache, rows, wout)


def ranks(targets, sources):
    count = targets.shape[0]
    one_hot = (targets[:, None] == jnp.arange(sources, dtype=jnp.int32)[None, :])
    rows = jnp.arange(count, dtype=jnp.int32)
    lower = (rows[None, :] < rows[:, None]).astype(jnp.bfloat16)
    earlier = jnp.dot(lower, one_hot.astype(jnp.bfloat16), preferred_element_type=jnp.float32)
    return jnp.sum(jnp.where(one_hot, earlier, 0.0), axis=1).astype(jnp.int32)


def block_plan(ints, half, n_half, per_pair, sources):
    picks, targets, places = ints[0], ints[1], ints[2]
    within = ranks(targets, sources)
    keep = (targets // n_half) == half
    position = jnp.where(keep, (targets % n_half) * per_pair + within, -1)
    spots = jnp.arange(n_half * per_pair, dtype=jnp.int32)
    hit = position[None, :] == spots[:, None]
    row = jnp.sum(jnp.where(hit, picks[None, :], 0), axis=1)
    slot = jnp.sum(jnp.where(hit, places[None, :] + 1, 0), axis=1) - 1
    return row.reshape(n_half, per_pair), slot.reshape(n_half, per_pair)


def select_rows(table, rows, slots):
    flat_rows = rows.reshape(-1)
    used = slots.reshape(-1) >= 0
    entries = jnp.arange(table.shape[0], dtype=jnp.int32)
    one_hot = ((flat_rows[:, None] == entries[None, :]) & used[:, None]).astype(table.dtype)
    picked = jnp.dot(one_hot, table, preferred_element_type=jnp.float32).astype(table.dtype)
    return picked.reshape(rows.shape + (table.shape[1],))


def shards(
    item_table,
    picked_items,
    destination,
    slot_index,
    history_cache,
    history_length,
    input_weight,
    output_weight,
):
    n_half = lax.axis_size("xy")
    sources = HALVES * n_half
    half = lax.axis_index("zh")
    item_rows = item_table[0, 0]
    ints = jnp.stack([picked_items[0, 0], destination[0, 0], slot_index[0, 0]])
    slot_count = ints.shape[1]
    feature = item_rows.shape[1]
    per_pair = 2 * slot_count // sources
    swap = [(0, 1), (1, 0)]
    other_rows = lax.ppermute(item_rows, "zh", swap)
    other_ints = lax.ppermute(ints, "zh", swap)

    own_row, own_slot = block_plan(ints, half, n_half, per_pair, sources)
    far_row, far_slot = block_plan(other_ints, half, n_half, per_pair, sources)
    own_data = select_rows(item_rows, own_row, own_slot)
    far_data = select_rows(other_rows, far_row, far_slot)
    slots = jnp.concatenate([own_slot, far_slot], axis=1)
    capacity = 2 * per_pair
    every_slot = lax.all_gather(slots, "xy", axis=0, tiled=False)
    tags = lax.dynamic_index_in_dim(every_slot, lax.axis_index("xy"), axis=1, keepdims=False)
    tags = tags.reshape(-1)
    outgoing = jnp.concatenate([own_data, far_data], axis=1)
    arrived = lax.all_to_all(outgoing, "xy", split_axis=0, concat_axis=0, tiled=True)
    arrived_rows = arrived.reshape(n_half * capacity, feature)
    slot_ids = jnp.arange(slot_count, dtype=jnp.int32)
    order = jnp.arange(n_half * capacity, dtype=jnp.int32)
    fill = jnp.sum(jnp.where(tags[None, :] == slot_ids[:, None], order[None, :], 0), axis=1)
    arranged = jnp.take(arrived_rows, fill, axis=0)

    lengths = history_length[0]
    as_float = arranged.astype(jnp.float32)
    normed_in = layer_norm(as_float).astype(jnp.bfloat16)
    projected = jax.nn.silu(
        jnp.dot(normed_in, input_weight, preferred_element_type=jnp.float32)
    ).astype(jnp.bfloat16)
    cache = lax.all_gather(history_cache, "cand", axis=1, tiled=True)[0]
    mixed = tail(lengths, projected, cache, arranged, output_weight)
    return mixed[None, None]


def solution(mesh):
    n_req, n_cand = mesh.devices.shape
    devices = mesh.devices.reshape(HALVES, n_req // HALVES, n_cand)
    split = Mesh(devices, ("zh", "xy", "cand"))
    req = ("zh", "xy")
    in_specs = (
        P(req, "cand", None, None),
        P(req, "cand", None),
        P(req, "cand", None),
        P(req, "cand", None),
        P(req, "cand", None, None),
        P(req, None),
        P(),
        P(),
    )
    out_specs = P(req, "cand", None, None)
    return jax.shard_map(shards, mesh=split, in_specs=in_specs, out_specs=out_specs, check_vma=False)
```

```python
import math

import functools

import jax
import jax.numpy as jnp
from jax import lax
from jax.experimental import pallas as pl
from jax.experimental.pallas import tpu as pltpu
from jax.sharding import Mesh
from jax.sharding import PartitionSpec as P

HEADS = 8
HALVES = 2


epsilon = 1e-06


def layer_norm(values):
    average = jnp.mean(values, axis=-1, keepdims=True)
    centred = values - average
    variance = jnp.mean(centred * centred, axis=-1, keepdims=True)
    return centred * lax.rsqrt(variance + epsilon)


def silu(v):
    return v / (1.0 + jnp.exp(-v))

def tail_kernel(len_ref, proj_ref, cache_ref, rows_ref, wout_ref, out_ref, att_ref, *, heads, eps):
    b = pl.program_id(0)
    feature = rows_ref.shape[1]
    head_width = feature // heads
    hist = cache_ref.shape[1]
    scale = 1.0 / math.sqrt(head_width)
    length = len_ref[b]
    length_plus = length.astype(jnp.float32) + 1.0
    valid = lax.broadcasted_iota(jnp.int32, (1, hist), 1) < length
    for h in range(heads):
        lo = h * head_width
        q = proj_ref[:, 2 * feature + lo : 2 * feature + lo + head_width]
        k = cache_ref[0, :, lo : lo + head_width]
        v = cache_ref[0, :, feature + lo : feature + lo + head_width]
        s = lax.dot_general(q, k, (((1,), (1,)), ((), ())), preferred_element_type=jnp.float32) * scale
        w = jnp.where(valid, silu(s) / length_plus, 0.0).astype(jnp.bfloat16)
        found = jnp.dot(w, v, preferred_element_type=jnp.float32)
        own_k = proj_ref[:, 3 * feature + lo : 3 * feature + lo + head_width].astype(jnp.float32)
        own_v = proj_ref[:, feature + lo : feature + lo + head_width].astype(jnp.float32)
        own_s = jnp.sum(q.astype(jnp.float32) * own_k, axis=-1, keepdims=True) * scale
        att_ref[:, lo : lo + head_width] = found + (silu(own_s) / length_plus) * own_v
    att = att_ref[...]
    mean = jnp.mean(att, axis=-1, keepdims=True)
    centred = att - mean
    var = jnp.mean(centred * centred, axis=-1, keepdims=True)
    normed = centred * lax.rsqrt(var + eps)
    gated = (normed * proj_ref[:, 0:feature].astype(jnp.float32)).astype(jnp.bfloat16)
    update = jnp.dot(gated, wout_ref[...], preferred_element_type=jnp.float32)
    out_ref[...] = (rows_ref[...].astype(jnp.float32) + update).astype(out_ref.dtype)

def tail(lengths, projected, cache, rows, wout, heads=8, eps=1e-6):
    members, hist, doubled = cache.shape
    slots, feature = rows.shape
    per = slots // members
    width = projected.shape[1]
    kern = functools.partial(tail_kernel, heads=heads, eps=eps)
    spec = pltpu.PrefetchScalarGridSpec(
        num_scalar_prefetch=1, grid=(members,),
        in_specs=[pl.BlockSpec((per, width), lambda b, n: (b, 0)),
                  pl.BlockSpec((1, hist, doubled), lambda b, n: (b, 0, 0)),
                  pl.BlockSpec((per, feature), lambda b, n: (b, 0)),
                  pl.BlockSpec((feature, feature), lambda b, n: (0, 0))],
        out_specs=pl.BlockSpec((per, feature), lambda b, n: (b, 0)),
        scratch_shapes=[pltpu.VMEM((per, feature), jnp.float32)])
    return pl.pallas_call(kern, grid_spec=spec, out_shape=jax.ShapeDtypeStruct((slots, feature), jnp.bfloat16),
        cost_estimate=pl.CostEstimate(flops=2*slots*feature*feature + 4*slots*hist*feature, transcendentals=slots*(hist*heads+heads), bytes_accessed=slots*width*2 + members*hist*doubled*2 + 2*slots*feature*2 + feature*feature*2))(lengths, projected, cache, rows, wout)


def ranks(targets, sources):
    count = targets.shape[0]
    one_hot = (targets[:, None] == jnp.arange(sources, dtype=jnp.int32)[None, :])
    rows = jnp.arange(count, dtype=jnp.int32)
    lower = (rows[None, :] < rows[:, None]).astype(jnp.bfloat16)
    earlier = jnp.dot(lower, one_hot.astype(jnp.bfloat16), preferred_element_type=jnp.float32)
    return jnp.sum(jnp.where(one_hot, earlier, 0.0), axis=1).astype(jnp.int32)


def block_plan(ints, half, n_half, per_pair, sources):
    picks, targets, places = ints[0], ints[1], ints[2]
    within = ranks(targets, sources)
    keep = (targets // n_half) == half
    position = jnp.where(keep, (targets % n_half) * per_pair + within, -1)
    spots = jnp.arange(n_half * per_pair, dtype=jnp.int32)
    hit = position[None, :] == spots[:, None]
    row = jnp.sum(jnp.where(hit, picks[None, :], 0), axis=1)
    slot = jnp.sum(jnp.where(hit, places[None, :] + 1, 0), axis=1) - 1
    return row.reshape(n_half, per_pair), slot.reshape(n_half, per_pair)


def select_rows(table, rows, slots):
    flat_rows = rows.reshape(-1)
    used = slots.reshape(-1) >= 0
    entries = jnp.arange(table.shape[0], dtype=jnp.int32)
    one_hot = ((flat_rows[:, None] == entries[None, :]) & used[:, None]).astype(table.dtype)
    picked = jnp.dot(one_hot, table, preferred_element_type=jnp.float32).astype(table.dtype)
    return picked.reshape(rows.shape + (table.shape[1],))


def place_rows(arrived, tags, slot_ids):
    rows = arrived.reshape(-1, arrived.shape[-1])
    one_hot = (slot_ids[:, None] == tags.reshape(-1)[None, :]).astype(rows.dtype)
    return jnp.dot(one_hot, rows, preferred_element_type=jnp.float32)


def shards(
    item_table,
    picked_items,
    destination,
    slot_index,
    history_cache,
    history_length,
    input_weight,
    output_weight,
):
    n_half = lax.axis_size("xy")
    sources = HALVES * n_half
    half = lax.axis_index("zh")
    item_rows = item_table[0, 0]
    ints = jnp.stack([picked_items[0, 0], destination[0, 0], slot_index[0, 0]])
    slot_count = ints.shape[1]
    feature = item_rows.shape[1]
    per_pair = 2 * slot_count // sources
    swap = [(0, 1), (1, 0)]
    other_rows = lax.ppermute(item_rows, "zh", swap)
    other_ints = lax.ppermute(ints, "zh", swap)

    own_row, own_slot = block_plan(ints, half, n_half, per_pair, sources)
    far_row, far_slot = block_plan(other_ints, half, n_half, per_pair, sources)
    own_data = select_rows(item_rows, own_row, own_slot)
    far_data = select_rows(other_rows, far_row, far_slot)
    slots = jnp.concatenate([own_slot, far_slot], axis=1)
    capacity = 2 * per_pair
    every_slot = lax.all_gather(slots, "xy", axis=0, tiled=False)
    tags = lax.dynamic_index_in_dim(every_slot, lax.axis_index("xy"), axis=1, keepdims=False)
    tags = tags.reshape(-1)
    own_arrived = lax.all_to_all(own_data, "xy", split_axis=0, concat_axis=0, tiled=True)
    far_arrived = lax.all_to_all(far_data, "xy", split_axis=0, concat_axis=0, tiled=True)
    slot_ids = jnp.arange(slot_count, dtype=jnp.int32)
    tags = tags.reshape(n_half, 2, per_pair)
    as_float = place_rows(own_arrived, tags[:, 0], slot_ids) + place_rows(
        far_arrived, tags[:, 1], slot_ids
    )
    arranged = as_float.astype(jnp.bfloat16)

    lengths = history_length[0]
    normed_in = layer_norm(as_float).astype(jnp.bfloat16)
    projected = jax.nn.silu(
        jnp.dot(normed_in, input_weight, preferred_element_type=jnp.float32)
    ).astype(jnp.bfloat16)
    cache = lax.all_gather(history_cache, "cand", axis=1, tiled=True)[0]
    mixed = tail(lengths, projected, cache, arranged, output_weight)
    return mixed[None, None]


def solution(mesh):
    n_req, n_cand = mesh.devices.shape
    devices = mesh.devices.reshape(HALVES, n_req // HALVES, n_cand)
    split = Mesh(devices, ("zh", "xy", "cand"))
    req = ("zh", "xy")
    in_specs = (
        P(req, "cand", None, None),
        P(req, "cand", None),
        P(req, "cand", None),
        P(req, "cand", None),
        P(req, "cand", None, None),
        P(req, None),
        P(),
        P(),
    )
    out_specs = P(req, "cand", None, None)
    return jax.shard_map(shards, mesh=split, in_specs=in_specs, out_specs=out_specs, check_vma=False)
```

```python
import math

import functools

import jax
import jax.numpy as jnp
from jax import lax
from jax.experimental import pallas as pl
from jax.experimental.pallas import tpu as pltpu
from jax.sharding import Mesh
from jax.sharding import PartitionSpec as P

HEADS = 8
HALVES = 2


epsilon = 1e-06


def layer_norm(values):
    average = jnp.mean(values, axis=-1, keepdims=True)
    centred = values - average
    variance = jnp.mean(centred * centred, axis=-1, keepdims=True)
    return centred * lax.rsqrt(variance + epsilon)


def silu(v):
    return v / (1.0 + jnp.exp(-v))

def tail_kernel(len_ref, proj_ref, cache_ref, rows_ref, wout_ref, out_ref, att_ref, *, heads, eps):
    step = pl.program_id(0)
    group, hist, doubled = cache_ref.shape
    per = rows_ref.shape[0] // group
    feature = rows_ref.shape[1]
    head_width = feature // heads
    scale = 1.0 / math.sqrt(head_width)
    for member in range(group):
        length = len_ref[step * group + member]
        inverse = 1.0 / (length.astype(jnp.float32) + 1.0)
        valid = lax.broadcasted_iota(jnp.int32, (1, hist), 1) < length
        rows = pl.ds(member * per, per)
        for h in range(heads):
            lo = h * head_width
            q = proj_ref[rows, 2 * feature + lo : 2 * feature + lo + head_width]
            k = cache_ref[member, :, lo : lo + head_width]
            v = cache_ref[member, :, feature + lo : feature + lo + head_width]
            s = lax.dot_general(q, k, (((1,), (1,)), ((), ())), preferred_element_type=jnp.float32) * scale
            w = jnp.where(valid, silu(s) * inverse, 0.0).astype(jnp.bfloat16)
            found = jnp.dot(w, v, preferred_element_type=jnp.float32)
            own_k = proj_ref[rows, 3 * feature + lo : 3 * feature + lo + head_width].astype(jnp.float32)
            own_v = proj_ref[rows, feature + lo : feature + lo + head_width].astype(jnp.float32)
            own_s = jnp.sum(q.astype(jnp.float32) * own_k, axis=-1, keepdims=True) * scale
            att_ref[rows, lo : lo + head_width] = found + (silu(own_s) * inverse) * own_v
    att = att_ref[...]
    mean = jnp.mean(att, axis=-1, keepdims=True)
    centred = att - mean
    var = jnp.mean(centred * centred, axis=-1, keepdims=True)
    normed = centred * lax.rsqrt(var + eps)
    gated = (normed * proj_ref[:, 0:feature].astype(jnp.float32)).astype(jnp.bfloat16)
    update = jnp.dot(gated, wout_ref[...], preferred_element_type=jnp.float32)
    out_ref[...] = (rows_ref[...].astype(jnp.float32) + update).astype(out_ref.dtype)

def tail(lengths, projected, cache, rows, wout, heads=8, eps=1e-6, group=2):
    members, hist, doubled = cache.shape
    slots, feature = rows.shape
    per = slots // members * group
    width = projected.shape[1]
    kern = functools.partial(tail_kernel, heads=heads, eps=eps)
    spec = pltpu.PrefetchScalarGridSpec(
        num_scalar_prefetch=1, grid=(members // group,),
        in_specs=[pl.BlockSpec((per, width), lambda b, n: (b, 0)),
                  pl.BlockSpec((group, hist, doubled), lambda b, n: (b, 0, 0)),
                  pl.BlockSpec((per, feature), lambda b, n: (b, 0)),
                  pl.BlockSpec((feature, feature), lambda b, n: (0, 0))],
        out_specs=pl.BlockSpec((per, feature), lambda b, n: (b, 0)),
        scratch_shapes=[pltpu.VMEM((per, feature), jnp.float32)])
    return pl.pallas_call(kern, grid_spec=spec, out_shape=jax.ShapeDtypeStruct((slots, feature), jnp.bfloat16),
        cost_estimate=pl.CostEstimate(flops=2*slots*feature*feature + 4*slots*hist*feature, transcendentals=slots*(hist*heads+heads), bytes_accessed=slots*width*2 + members*hist*doubled*2 + 2*slots*feature*2 + feature*feature*2))(lengths, projected, cache, rows, wout)


def ranks(targets, sources):
    count = targets.shape[0]
    one_hot = (targets[:, None] == jnp.arange(sources, dtype=jnp.int32)[None, :])
    rows = jnp.arange(count, dtype=jnp.int32)
    lower = (rows[None, :] < rows[:, None]).astype(jnp.bfloat16)
    earlier = jnp.dot(lower, one_hot.astype(jnp.bfloat16), preferred_element_type=jnp.float32)
    return jnp.sum(jnp.where(one_hot, earlier, 0.0), axis=1).astype(jnp.int32)


def block_plan(ints, half, n_half, per_pair, sources):
    picks, targets, places = ints[0], ints[1], ints[2]
    within = ranks(targets, sources)
    keep = (targets // n_half) == half
    position = jnp.where(keep, (targets % n_half) * per_pair + within, -1)
    spots = jnp.arange(n_half * per_pair, dtype=jnp.int32)
    hit = position[None, :] == spots[:, None]
    row = jnp.sum(jnp.where(hit, picks[None, :], 0), axis=1)
    slot = jnp.sum(jnp.where(hit, places[None, :] + 1, 0), axis=1) - 1
    return row.reshape(n_half, per_pair), slot.reshape(n_half, per_pair)


def select_rows(table, rows, slots):
    flat_rows = rows.reshape(-1)
    used = slots.reshape(-1) >= 0
    entries = jnp.arange(table.shape[0], dtype=jnp.int32)
    one_hot = ((flat_rows[:, None] == entries[None, :]) & used[:, None]).astype(table.dtype)
    picked = jnp.dot(one_hot, table, preferred_element_type=jnp.float32).astype(table.dtype)
    return picked.reshape(rows.shape + (table.shape[1],))


def place_rows(arrived, tags, slot_ids):
    rows = arrived.reshape(-1, arrived.shape[-1])
    one_hot = (slot_ids[:, None] == tags.reshape(-1)[None, :]).astype(rows.dtype)
    return jnp.dot(one_hot, rows, preferred_element_type=jnp.float32)


def shards(
    item_table,
    picked_items,
    destination,
    slot_index,
    history_cache,
    history_length,
    input_weight,
    output_weight,
):
    n_half = lax.axis_size("xy")
    sources = HALVES * n_half
    half = lax.axis_index("zh")
    item_rows = item_table[0, 0]
    ints = jnp.stack([picked_items[0, 0], destination[0, 0], slot_index[0, 0]])
    slot_count = ints.shape[1]
    feature = item_rows.shape[1]
    per_pair = 2 * slot_count // sources
    swap = [(0, 1), (1, 0)]
    other_rows = lax.ppermute(item_rows, "zh", swap)
    other_ints = lax.ppermute(ints, "zh", swap)

    own_row, own_slot = block_plan(ints, half, n_half, per_pair, sources)
    far_row, far_slot = block_plan(other_ints, half, n_half, per_pair, sources)
    own_data = select_rows(item_rows, own_row, own_slot)
    far_data = select_rows(other_rows, far_row, far_slot)
    slots = jnp.concatenate([own_slot, far_slot], axis=1)
    capacity = 2 * per_pair
    every_slot = lax.all_gather(slots, "xy", axis=0, tiled=False)
    tags = lax.dynamic_index_in_dim(every_slot, lax.axis_index("xy"), axis=1, keepdims=False)
    tags = tags.reshape(-1)
    own_arrived = lax.all_to_all(own_data, "xy", split_axis=0, concat_axis=0, tiled=True)
    tags, far_data = lax.optimization_barrier((tags, far_data))
    far_arrived = lax.all_to_all(far_data, "xy", split_axis=0, concat_axis=0, tiled=True)
    slot_ids = jnp.arange(slot_count, dtype=jnp.int32)
    tags = tags.reshape(n_half, 2, per_pair)
    as_float = place_rows(own_arrived, tags[:, 0], slot_ids) + place_rows(
        far_arrived, tags[:, 1], slot_ids
    )
    arranged = as_float.astype(jnp.bfloat16)

    lengths = history_length[0]
    normed_in = layer_norm(as_float).astype(jnp.bfloat16)
    projected = jax.nn.silu(
        jnp.dot(normed_in, input_weight, preferred_element_type=jnp.float32)
    ).astype(jnp.bfloat16)
    cache = lax.all_gather(history_cache, "cand", axis=1, tiled=True)[0]
    mixed = tail(lengths, projected, cache, arranged, output_weight)
    return mixed[None, None]


def solution(mesh):
    n_req, n_cand = mesh.devices.shape
    devices = mesh.devices.reshape(HALVES, n_req // HALVES, n_cand)
    split = Mesh(devices, ("zh", "xy", "cand"))
    req = ("zh", "xy")
    in_specs = (
        P(req, "cand", None, None),
        P(req, "cand", None),
        P(req, "cand", None),
        P(req, "cand", None),
        P(req, "cand", None, None),
        P(req, None),
        P(),
        P(),
    )
    out_specs = P(req, "cand", None, None)
    return jax.shard_map(shards, mesh=split, in_specs=in_specs, out_specs=out_specs, check_vma=False)
```

```python
import math

import functools

import jax
import jax.numpy as jnp
from jax import lax
from jax.experimental import pallas as pl
from jax.experimental.pallas import tpu as pltpu
from jax.sharding import Mesh
from jax.sharding import PartitionSpec as P

HEADS = 8
HALVES = 2


epsilon = 1e-06


def layer_norm(values):
    average = jnp.mean(values, axis=-1, keepdims=True)
    centred = values - average
    variance = jnp.mean(centred * centred, axis=-1, keepdims=True)
    return centred * lax.rsqrt(variance + epsilon)


def silu(v):
    return v * (0.5 + 0.5 * jnp.tanh(0.5 * v))

def tail_kernel(len_ref, proj_ref, cache_ref, rows_ref, wout_ref, out_ref, att_ref, *, heads, eps):
    step = pl.program_id(0)
    group, hist, doubled = cache_ref.shape
    per = rows_ref.shape[0] // group
    feature = rows_ref.shape[1]
    head_width = feature // heads
    scale = 1.0 / math.sqrt(head_width)
    for member in range(group):
        length = len_ref[step * group + member]
        inverse = 1.0 / (length.astype(jnp.float32) + 1.0)
        valid = lax.broadcasted_iota(jnp.int32, (1, hist), 1) < length
        rows = pl.ds(member * per, per)
        for h in range(heads):
            lo = h * head_width
            q = proj_ref[rows, 2 * feature + lo : 2 * feature + lo + head_width]
            k = cache_ref[member, :, lo : lo + head_width]
            v = cache_ref[member, :, feature + lo : feature + lo + head_width]
            s = lax.dot_general(q, k, (((1,), (1,)), ((), ())), preferred_element_type=jnp.float32) * scale
            w = jnp.where(valid, silu(s) * inverse, 0.0).astype(jnp.bfloat16)
            found = jnp.dot(w, v, preferred_element_type=jnp.float32)
            own_k = proj_ref[rows, 3 * feature + lo : 3 * feature + lo + head_width].astype(jnp.float32)
            own_v = proj_ref[rows, feature + lo : feature + lo + head_width].astype(jnp.float32)
            own_s = jnp.sum(q.astype(jnp.float32) * own_k, axis=-1, keepdims=True) * scale
            att_ref[rows, lo : lo + head_width] = found + (silu(own_s) * inverse) * own_v
    att = att_ref[...]
    mean = jnp.mean(att, axis=-1, keepdims=True)
    centred = att - mean
    var = jnp.mean(centred * centred, axis=-1, keepdims=True)
    normed = centred * lax.rsqrt(var + eps)
    gated = (normed * proj_ref[:, 0:feature].astype(jnp.float32)).astype(jnp.bfloat16)
    update = jnp.dot(gated, wout_ref[...], preferred_element_type=jnp.float32)
    out_ref[...] = (rows_ref[...].astype(jnp.float32) + update).astype(out_ref.dtype)

def tail(lengths, projected, cache, rows, wout, heads=8, eps=1e-6, group=2):
    members, hist, doubled = cache.shape
    slots, feature = rows.shape
    per = slots // members * group
    width = projected.shape[1]
    kern = functools.partial(tail_kernel, heads=heads, eps=eps)
    spec = pltpu.PrefetchScalarGridSpec(
        num_scalar_prefetch=1, grid=(members // group,),
        in_specs=[pl.BlockSpec((per, width), lambda b, n: (b, 0)),
                  pl.BlockSpec((group, hist, doubled), lambda b, n: (b, 0, 0)),
                  pl.BlockSpec((per, feature), lambda b, n: (b, 0)),
                  pl.BlockSpec((feature, feature), lambda b, n: (0, 0))],
        out_specs=pl.BlockSpec((per, feature), lambda b, n: (b, 0)),
        scratch_shapes=[pltpu.VMEM((per, feature), jnp.float32)])
    return pl.pallas_call(kern, grid_spec=spec, out_shape=jax.ShapeDtypeStruct((slots, feature), jnp.bfloat16),
        cost_estimate=pl.CostEstimate(flops=2*slots*feature*feature + 4*slots*hist*feature, transcendentals=slots*(hist*heads+heads), bytes_accessed=slots*width*2 + members*hist*doubled*2 + 2*slots*feature*2 + feature*feature*2))(lengths, projected, cache, rows, wout)


def ranks(targets, sources):
    count = targets.shape[0]
    one_hot = (targets[:, None] == jnp.arange(sources, dtype=jnp.int32)[None, :])
    rows = jnp.arange(count, dtype=jnp.int32)
    lower = (rows[None, :] < rows[:, None]).astype(jnp.bfloat16)
    earlier = jnp.dot(lower, one_hot.astype(jnp.bfloat16), preferred_element_type=jnp.float32)
    return jnp.sum(jnp.where(one_hot, earlier, 0.0), axis=1).astype(jnp.int32)


def block_plan(ints, half, n_half, per_pair, sources):
    picks, targets, places = ints[0], ints[1], ints[2]
    within = ranks(targets, sources)
    keep = (targets // n_half) == half
    position = jnp.where(keep, (targets % n_half) * per_pair + within, -1)
    spots = jnp.arange(n_half * per_pair, dtype=jnp.int32)
    hit = position[None, :] == spots[:, None]
    row = jnp.sum(jnp.where(hit, picks[None, :], 0), axis=1)
    slot = jnp.sum(jnp.where(hit, places[None, :] + 1, 0), axis=1) - 1
    return row.reshape(n_half, per_pair), slot.reshape(n_half, per_pair)


def select_rows(table, rows, slots):
    flat_rows = rows.reshape(-1)
    used = slots.reshape(-1) >= 0
    entries = jnp.arange(table.shape[0], dtype=jnp.int32)
    one_hot = ((flat_rows[:, None] == entries[None, :]) & used[:, None]).astype(table.dtype)
    picked = jnp.dot(one_hot, table, preferred_element_type=jnp.float32).astype(table.dtype)
    return picked.reshape(rows.shape + (table.shape[1],))


RADIX = 32
TAG_LANES = 128


def with_tags(data, slots):
    high = jnp.floor_divide(slots, RADIX)
    low = slots - high * RADIX
    lane = lax.broadcasted_iota(jnp.int32, slots.shape + (TAG_LANES,), 2)
    tags = jnp.where(lane == 0, high[..., None], jnp.where(lane == 1, low[..., None], 0))
    return jnp.concatenate([data, tags.astype(data.dtype)], axis=-1)


def place_rows(arrived, slot_ids, feature):
    rows = arrived.reshape(-1, arrived.shape[-1])
    tags = rows[:, feature].astype(jnp.int32) * RADIX + rows[:, feature + 1].astype(jnp.int32)
    one_hot = (slot_ids[:, None] == tags[None, :]).astype(rows.dtype)
    return jnp.dot(one_hot, rows[:, :feature], preferred_element_type=jnp.float32)


def shards(
    item_table,
    picked_items,
    destination,
    slot_index,
    history_cache,
    history_length,
    input_weight,
    output_weight,
):
    n_half = lax.axis_size("xy")
    sources = HALVES * n_half
    half = lax.axis_index("zh")
    item_rows = item_table[0, 0]
    ints = jnp.stack([picked_items[0, 0], destination[0, 0], slot_index[0, 0]])
    slot_count = ints.shape[1]
    feature = item_rows.shape[1]
    per_pair = 2 * slot_count // sources
    swap = [(0, 1), (1, 0)]
    other_rows = lax.ppermute(item_rows, "zh", swap)
    other_ints = lax.ppermute(ints, "zh", swap)

    own_row, own_slot = block_plan(ints, half, n_half, per_pair, sources)
    far_row, far_slot = block_plan(other_ints, half, n_half, per_pair, sources)
    own_data = select_rows(item_rows, own_row, own_slot)
    far_data = select_rows(other_rows, far_row, far_slot)
    own_arrived = lax.all_to_all(
        with_tags(own_data, own_slot), "xy", split_axis=0, concat_axis=0, tiled=True
    )
    far_arrived = lax.all_to_all(
        with_tags(far_data, far_slot), "xy", split_axis=0, concat_axis=0, tiled=True
    )
    slot_ids = jnp.arange(slot_count, dtype=jnp.int32)
    as_float = place_rows(own_arrived, slot_ids, feature) + place_rows(
        far_arrived, slot_ids, feature
    )
    arranged = as_float.astype(jnp.bfloat16)

    lengths = history_length[0]
    normed_in = layer_norm(as_float).astype(jnp.bfloat16)
    projected = jax.nn.silu(
        jnp.dot(normed_in, input_weight, preferred_element_type=jnp.float32)
    ).astype(jnp.bfloat16)
    cache = lax.all_gather(history_cache, "cand", axis=1, tiled=True)[0]
    mixed = tail(lengths, projected, cache, arranged, output_weight)
    return mixed[None, None]


def solution(mesh):
    n_req, n_cand = mesh.devices.shape
    devices = mesh.devices.reshape(HALVES, n_req // HALVES, n_cand)
    split = Mesh(devices, ("zh", "xy", "cand"))
    req = ("zh", "xy")
    in_specs = (
        P(req, "cand", None, None),
        P(req, "cand", None),
        P(req, "cand", None),
        P(req, "cand", None),
        P(req, "cand", None, None),
        P(req, None),
        P(),
        P(),
    )
    out_specs = P(req, "cand", None, None)
    return jax.shard_map(shards, mesh=split, in_specs=in_specs, out_specs=out_specs, check_vma=False)
```

```python
import math

import functools

import jax
import jax.numpy as jnp
from jax import lax
from jax.experimental import pallas as pl
from jax.experimental.pallas import tpu as pltpu
from jax.sharding import Mesh
from jax.sharding import PartitionSpec as P

HEADS = 8
HALVES = 2


epsilon = 1e-06


def layer_norm(values):
    average = jnp.mean(values, axis=-1, keepdims=True)
    centred = values - average
    variance = jnp.mean(centred * centred, axis=-1, keepdims=True)
    return centred * lax.rsqrt(variance + epsilon)


def silu(v):
    return v / (1.0 + jnp.exp(-v))

def tail_kernel(len_ref, proj_ref, cache_ref, rows_ref, wout_ref, out_ref, att_ref, *, heads, eps):
    step = pl.program_id(0)
    group, hist, doubled = cache_ref.shape
    per = rows_ref.shape[0] // group
    feature = rows_ref.shape[1]
    head_width = feature // heads
    scale = 1.0 / math.sqrt(head_width)
    for member in range(group):
        length = len_ref[step * group + member]
        inverse = 1.0 / (length.astype(jnp.float32) + 1.0)
        valid = lax.broadcasted_iota(jnp.int32, (1, hist), 1) < length
        rows = pl.ds(member * per, per)
        for h in range(heads):
            lo = h * head_width
            q = proj_ref[rows, 2 * feature + lo : 2 * feature + lo + head_width]
            k = cache_ref[member, :, lo : lo + head_width]
            v = cache_ref[member, :, feature + lo : feature + lo + head_width]
            s = lax.dot_general(q, k, (((1,), (1,)), ((), ())), preferred_element_type=jnp.float32) * scale
            w = jnp.where(valid, silu(s) * inverse, 0.0).astype(jnp.bfloat16)
            found = jnp.dot(w, v, preferred_element_type=jnp.float32)
            own_k = proj_ref[rows, 3 * feature + lo : 3 * feature + lo + head_width].astype(jnp.float32)
            own_v = proj_ref[rows, feature + lo : feature + lo + head_width].astype(jnp.float32)
            own_s = jnp.sum(q.astype(jnp.float32) * own_k, axis=-1, keepdims=True) * scale
            att_ref[rows, lo : lo + head_width] = found + (silu(own_s) * inverse) * own_v
    att = att_ref[...]
    mean = jnp.mean(att, axis=-1, keepdims=True)
    centred = att - mean
    var = jnp.mean(centred * centred, axis=-1, keepdims=True)
    normed = centred * lax.rsqrt(var + eps)
    gated = (normed * proj_ref[:, 0:feature].astype(jnp.float32)).astype(jnp.bfloat16)
    update = jnp.dot(gated, wout_ref[...], preferred_element_type=jnp.float32)
    out_ref[...] = (rows_ref[...].astype(jnp.float32) + update).astype(out_ref.dtype)

def tail(lengths, projected, cache, rows, wout, heads=8, eps=1e-6, group=2):
    members, hist, doubled = cache.shape
    slots, feature = rows.shape
    per = slots // members * group
    width = projected.shape[1]
    kern = functools.partial(tail_kernel, heads=heads, eps=eps)
    spec = pltpu.PrefetchScalarGridSpec(
        num_scalar_prefetch=1, grid=(members // group,),
        in_specs=[pl.BlockSpec((per, width), lambda b, n: (b, 0)),
                  pl.BlockSpec((group, hist, doubled), lambda b, n: (b, 0, 0)),
                  pl.BlockSpec((per, feature), lambda b, n: (b, 0)),
                  pl.BlockSpec((feature, feature), lambda b, n: (0, 0))],
        out_specs=pl.BlockSpec((per, feature), lambda b, n: (b, 0)),
        scratch_shapes=[pltpu.VMEM((per, feature), jnp.float32)])
    return pl.pallas_call(kern, grid_spec=spec, out_shape=jax.ShapeDtypeStruct((slots, feature), jnp.bfloat16),
        cost_estimate=pl.CostEstimate(flops=2*slots*feature*feature + 4*slots*hist*feature, transcendentals=slots*(hist*heads+heads), bytes_accessed=slots*width*2 + members*hist*doubled*2 + 2*slots*feature*2 + feature*feature*2))(lengths, projected, cache, rows, wout)


def ranks(targets, sources):
    count = targets.shape[0]
    one_hot = (targets[:, None] == jnp.arange(sources, dtype=jnp.int32)[None, :])
    rows = jnp.arange(count, dtype=jnp.int32)
    lower = (rows[None, :] < rows[:, None]).astype(jnp.bfloat16)
    earlier = jnp.dot(lower, one_hot.astype(jnp.bfloat16), preferred_element_type=jnp.float32)
    return jnp.sum(jnp.where(one_hot, earlier, 0.0), axis=1).astype(jnp.int32)


def block_plan(ints, half, n_half, per_pair, sources):
    picks, targets, places = ints[0], ints[1], ints[2]
    within = ranks(targets, sources)
    keep = (targets // n_half) == half
    position = jnp.where(keep, (targets % n_half) * per_pair + within, -1)
    spots = jnp.arange(n_half * per_pair, dtype=jnp.int32)
    hit = position[None, :] == spots[:, None]
    row = jnp.sum(jnp.where(hit, picks[None, :], 0), axis=1)
    slot = jnp.sum(jnp.where(hit, places[None, :] + 1, 0), axis=1) - 1
    return row.reshape(n_half, per_pair), slot.reshape(n_half, per_pair)


def select_rows(table, rows, slots):
    flat_rows = rows.reshape(-1)
    used = slots.reshape(-1) >= 0
    entries = jnp.arange(table.shape[0], dtype=jnp.int32)
    one_hot = ((flat_rows[:, None] == entries[None, :]) & used[:, None]).astype(table.dtype)
    picked = jnp.dot(one_hot, table, preferred_element_type=jnp.float32).astype(table.dtype)
    return picked.reshape(rows.shape + (table.shape[1],))


def place_rows(arrived, tags, slot_ids):
    rows = arrived.reshape(-1, arrived.shape[-1])
    one_hot = (slot_ids[:, None] == tags.reshape(-1)[None, :]).astype(rows.dtype)
    return jnp.dot(one_hot, rows, preferred_element_type=jnp.float32)


def shards(
    item_table,
    picked_items,
    destination,
    slot_index,
    history_cache,
    history_length,
    input_weight,
    output_weight,
):
    n_half = lax.axis_size("xy")
    sources = HALVES * n_half
    half = lax.axis_index("zh")
    item_rows = item_table[0, 0]
    ints = jnp.stack([picked_items[0, 0], destination[0, 0], slot_index[0, 0]])
    slot_count = ints.shape[1]
    feature = item_rows.shape[1]
    per_pair = 2 * slot_count // sources
    swap = [(0, 1), (1, 0)]
    other_rows = lax.ppermute(item_rows, "zh", swap)
    other_ints = lax.ppermute(ints, "zh", swap)

    own_row, own_slot = block_plan(ints, half, n_half, per_pair, sources)
    far_row, far_slot = block_plan(other_ints, half, n_half, per_pair, sources)
    own_data = select_rows(item_rows, own_row, own_slot)
    far_data = select_rows(other_rows, far_row, far_slot)
    sent_slot = block_plan(ints, 1 - half, n_half, per_pair, sources)[1]
    plans = jnp.stack([own_slot, sent_slot])
    every_plan = lax.all_gather(plans, ("zh", "xy"), axis=0, tiled=False)
    every_plan = every_plan.reshape((HALVES, n_half) + plans.shape)
    here = lax.axis_index("xy")
    own_tags = lax.dynamic_index_in_dim(every_plan[half, :, 0], here, axis=1, keepdims=False)
    far_tags = lax.dynamic_index_in_dim(every_plan[1 - half, :, 1], here, axis=1, keepdims=False)
    tags = jnp.stack([own_tags, far_tags], axis=1)
    tags, own_data = lax.optimization_barrier((tags, own_data))
    own_arrived = lax.all_to_all(own_data, "xy", split_axis=0, concat_axis=0, tiled=True)
    far_arrived = lax.all_to_all(far_data, "xy", split_axis=0, concat_axis=0, tiled=True)
    slot_ids = jnp.arange(slot_count, dtype=jnp.int32)
    as_float = place_rows(own_arrived, tags[:, 0], slot_ids) + place_rows(
        far_arrived, tags[:, 1], slot_ids
    )
    arranged = as_float.astype(jnp.bfloat16)

    lengths = history_length[0]
    normed_in = layer_norm(as_float).astype(jnp.bfloat16)
    projected = jax.nn.silu(
        jnp.dot(normed_in, input_weight, preferred_element_type=jnp.float32)
    ).astype(jnp.bfloat16)
    cache = lax.all_gather(history_cache, "cand", axis=1, tiled=True)[0]
    mixed = tail(lengths, projected, cache, arranged, output_weight)
    return mixed[None, None]


def solution(mesh):
    n_req, n_cand = mesh.devices.shape
    devices = mesh.devices.reshape(HALVES, n_req // HALVES, n_cand)
    split = Mesh(devices, ("zh", "xy", "cand"))
    req = ("zh", "xy")
    in_specs = (
        P(req, "cand", None, None),
        P(req, "cand", None),
        P(req, "cand", None),
        P(req, "cand", None),
        P(req, "cand", None, None),
        P(req, None),
        P(),
        P(),
    )
    out_specs = P(req, "cand", None, None)
    return jax.shard_map(shards, mesh=split, in_specs=in_specs, out_specs=out_specs, check_vma=False)
```

```python
import math

import functools

import jax
import jax.numpy as jnp
from jax import lax
from jax.experimental import pallas as pl
from jax.experimental.pallas import tpu as pltpu
from jax.sharding import Mesh
from jax.sharding import PartitionSpec as P

HEADS = 8
HALVES = 2


epsilon = 1e-06


def layer_norm(values):
    average = jnp.mean(values, axis=-1, keepdims=True)
    centred = values - average
    variance = jnp.mean(centred * centred, axis=-1, keepdims=True)
    return centred * lax.rsqrt(variance + epsilon)


def silu(v):
    return v / (1.0 + jnp.exp(-v))

def tail_kernel(len_ref, proj_ref, cache_ref, rows_ref, wout_ref, out_ref, att_ref, *, heads, eps):
    step = pl.program_id(0)
    group, hist, doubled = cache_ref.shape
    per = rows_ref.shape[0] // group
    feature = rows_ref.shape[1]
    head_width = feature // heads
    scale = 1.0 / math.sqrt(head_width)
    for member in range(group):
        length = len_ref[step * group + member]
        inverse = 1.0 / (length.astype(jnp.float32) + 1.0)
        valid = lax.broadcasted_iota(jnp.int32, (1, hist), 1) < length
        rows = pl.ds(member * per, per)
        for h in range(heads):
            lo = h * head_width
            q = proj_ref[rows, 2 * feature + lo : 2 * feature + lo + head_width]
            k = cache_ref[member, :, lo : lo + head_width]
            v = cache_ref[member, :, feature + lo : feature + lo + head_width]
            s = lax.dot_general(q, k, (((1,), (1,)), ((), ())), preferred_element_type=jnp.float32) * scale
            w = jnp.where(valid, silu(s) * inverse, 0.0).astype(jnp.bfloat16)
            found = jnp.dot(w, v, preferred_element_type=jnp.float32)
            own_k = proj_ref[rows, 3 * feature + lo : 3 * feature + lo + head_width].astype(jnp.float32)
            own_v = proj_ref[rows, feature + lo : feature + lo + head_width].astype(jnp.float32)
            own_s = jnp.sum(q.astype(jnp.float32) * own_k, axis=-1, keepdims=True) * scale
            att_ref[rows, lo : lo + head_width] = found + (silu(own_s) * inverse) * own_v
    att = att_ref[...]
    mean = jnp.mean(att, axis=-1, keepdims=True)
    centred = att - mean
    var = jnp.mean(centred * centred, axis=-1, keepdims=True)
    normed = centred * lax.rsqrt(var + eps)
    gated = (normed * proj_ref[:, 0:feature].astype(jnp.float32)).astype(jnp.bfloat16)
    update = jnp.dot(gated, wout_ref[...], preferred_element_type=jnp.float32)
    out_ref[...] = (rows_ref[...].astype(jnp.float32) + update).astype(out_ref.dtype)

def tail(lengths, projected, cache, rows, wout, heads=8, eps=1e-6, group=2):
    members, hist, doubled = cache.shape
    slots, feature = rows.shape
    per = slots // members * group
    width = projected.shape[1]
    kern = functools.partial(tail_kernel, heads=heads, eps=eps)
    spec = pltpu.PrefetchScalarGridSpec(
        num_scalar_prefetch=1, grid=(members // group,),
        in_specs=[pl.BlockSpec((per, width), lambda b, n: (b, 0)),
                  pl.BlockSpec((group, hist, doubled), lambda b, n: (b, 0, 0)),
                  pl.BlockSpec((per, feature), lambda b, n: (b, 0)),
                  pl.BlockSpec((feature, feature), lambda b, n: (0, 0))],
        out_specs=pl.BlockSpec((per, feature), lambda b, n: (b, 0)),
        scratch_shapes=[pltpu.VMEM((per, feature), jnp.float32)])
    return pl.pallas_call(kern, grid_spec=spec, out_shape=jax.ShapeDtypeStruct((slots, feature), jnp.bfloat16),
        cost_estimate=pl.CostEstimate(flops=2*slots*feature*feature + 4*slots*hist*feature, transcendentals=slots*(hist*heads+heads), bytes_accessed=slots*width*2 + members*hist*doubled*2 + 2*slots*feature*2 + feature*feature*2))(lengths, projected, cache, rows, wout)


def ranks(targets, sources):
    count = targets.shape[0]
    one_hot = (targets[:, None] == jnp.arange(sources, dtype=jnp.int32)[None, :])
    rows = jnp.arange(count, dtype=jnp.int32)
    lower = (rows[None, :] < rows[:, None]).astype(jnp.bfloat16)
    earlier = jnp.dot(lower, one_hot.astype(jnp.bfloat16), preferred_element_type=jnp.float32)
    return jnp.sum(jnp.where(one_hot, earlier, 0.0), axis=1).astype(jnp.int32)


def block_plan(ints, half, n_half, per_pair, sources):
    picks, targets, places = ints[0], ints[1], ints[2]
    within = ranks(targets, sources)
    keep = (targets // n_half) == half
    position = jnp.where(keep, (targets % n_half) * per_pair + within, -1)
    spots = jnp.arange(n_half * per_pair, dtype=jnp.int32)
    hit = position[None, :] == spots[:, None]
    row = jnp.sum(jnp.where(hit, picks[None, :], 0), axis=1)
    slot = jnp.sum(jnp.where(hit, places[None, :] + 1, 0), axis=1) - 1
    return row.reshape(n_half, per_pair), slot.reshape(n_half, per_pair)


def select_rows(table, rows, slots):
    flat_rows = rows.reshape(-1)
    used = slots.reshape(-1) >= 0
    entries = jnp.arange(table.shape[0], dtype=jnp.int32)
    one_hot = ((flat_rows[:, None] == entries[None, :]) & used[:, None]).astype(table.dtype)
    picked = jnp.dot(one_hot, table, preferred_element_type=jnp.float32).astype(table.dtype)
    return picked.reshape(rows.shape + (table.shape[1],))


def place_rows(arrived, tags, slot_ids):
    rows = arrived.reshape(-1, arrived.shape[-1])
    one_hot = (slot_ids[:, None] == tags.reshape(-1)[None, :]).astype(rows.dtype)
    return jnp.dot(one_hot, rows, preferred_element_type=jnp.float32)


def shards(
    item_table,
    picked_items,
    destination,
    slot_index,
    history_cache,
    history_length,
    input_weight,
    output_weight,
):
    n_half = lax.axis_size("xy")
    sources = HALVES * n_half
    half = lax.axis_index("zh")
    item_rows = item_table[0, 0]
    ints = jnp.stack([picked_items[0, 0], destination[0, 0], slot_index[0, 0]])
    slot_count = ints.shape[1]
    feature = item_rows.shape[1]
    per_pair = 2 * slot_count // sources
    swap = [(0, 1), (1, 0)]
    other_rows = lax.ppermute(item_rows, "zh", swap)
    other_ints = lax.ppermute(ints, "zh", swap)

    own_row, own_slot = block_plan(ints, half, n_half, per_pair, sources)
    far_row, far_slot = block_plan(other_ints, half, n_half, per_pair, sources)
    own_data = select_rows(item_rows, own_row, own_slot)
    far_data = select_rows(other_rows, far_row, far_slot)
    slots = jnp.concatenate([own_slot, far_slot], axis=1)
    capacity = 2 * per_pair
    tags = lax.all_to_all(slots, "xy", split_axis=0, concat_axis=0, tiled=True)
    tags = tags.reshape(-1)
    own_arrived = lax.all_to_all(own_data, "xy", split_axis=0, concat_axis=0, tiled=True)
    tags, far_data = lax.optimization_barrier((tags, far_data))
    far_arrived = lax.all_to_all(far_data, "xy", split_axis=0, concat_axis=0, tiled=True)
    slot_ids = jnp.arange(slot_count, dtype=jnp.int32)
    tags = tags.reshape(n_half, 2, per_pair)
    as_float = place_rows(own_arrived, tags[:, 0], slot_ids) + place_rows(
        far_arrived, tags[:, 1], slot_ids
    )
    arranged = as_float.astype(jnp.bfloat16)

    lengths = history_length[0]
    normed_in = layer_norm(as_float).astype(jnp.bfloat16)
    projected = jax.nn.silu(
        jnp.dot(normed_in, input_weight, preferred_element_type=jnp.float32)
    ).astype(jnp.bfloat16)
    cache = lax.all_gather(history_cache, "cand", axis=1, tiled=True)[0]
    mixed = tail(lengths, projected, cache, arranged, output_weight)
    return mixed[None, None]


def solution(mesh):
    n_req, n_cand = mesh.devices.shape
    devices = mesh.devices.reshape(HALVES, n_req // HALVES, n_cand)
    split = Mesh(devices, ("zh", "xy", "cand"))
    req = ("zh", "xy")
    in_specs = (
        P(req, "cand", None, None),
        P(req, "cand", None),
        P(req, "cand", None),
        P(req, "cand", None),
        P(req, "cand", None, None),
        P(req, None),
        P(),
        P(),
    )
    out_specs = P(req, "cand", None, None)
    return jax.shard_map(shards, mesh=split, in_specs=in_specs, out_specs=out_specs, check_vma=False)
```

```python
import math

import functools

import jax
import jax.numpy as jnp
from jax import lax
from jax.experimental import pallas as pl
from jax.experimental.pallas import tpu as pltpu
from jax.sharding import Mesh
from jax.sharding import PartitionSpec as P

HEADS = 8
HALVES = 2
RADIX = 32
CODE_ROWS = 16


epsilon = 1e-06


def layer_norm(values):
    average = jnp.mean(values, axis=-1, keepdims=True)
    centred = values - average
    variance = jnp.mean(centred * centred, axis=-1, keepdims=True)
    return centred * lax.rsqrt(variance + epsilon)


def silu(v):
    return v / (1.0 + jnp.exp(-v))

def tail_kernel(len_ref, proj_ref, cache_ref, rows_ref, wout_ref, out_ref, att_ref, *, heads, eps):
    step = pl.program_id(0)
    group, hist, doubled = cache_ref.shape
    per = rows_ref.shape[0] // group
    feature = rows_ref.shape[1]
    head_width = feature // heads
    scale = 1.0 / math.sqrt(head_width)
    for member in range(group):
        length = len_ref[step * group + member]
        inverse = 1.0 / (length.astype(jnp.float32) + 1.0)
        valid = lax.broadcasted_iota(jnp.int32, (1, hist), 1) < length
        rows = pl.ds(member * per, per)
        for h in range(heads):
            lo = h * head_width
            q = proj_ref[rows, 2 * feature + lo : 2 * feature + lo + head_width]
            k = cache_ref[member, :, lo : lo + head_width]
            v = cache_ref[member, :, feature + lo : feature + lo + head_width]
            s = lax.dot_general(q, k, (((1,), (1,)), ((), ())), preferred_element_type=jnp.float32) * scale
            w = jnp.where(valid, silu(s) * inverse, 0.0).astype(jnp.bfloat16)
            found = jnp.dot(w, v, preferred_element_type=jnp.float32)
            own_k = proj_ref[rows, 3 * feature + lo : 3 * feature + lo + head_width].astype(jnp.float32)
            own_v = proj_ref[rows, feature + lo : feature + lo + head_width].astype(jnp.float32)
            own_s = jnp.sum(q.astype(jnp.float32) * own_k, axis=-1, keepdims=True) * scale
            att_ref[rows, lo : lo + head_width] = found + (silu(own_s) * inverse) * own_v
    att = att_ref[...]
    mean = jnp.mean(att, axis=-1, keepdims=True)
    centred = att - mean
    var = jnp.mean(centred * centred, axis=-1, keepdims=True)
    normed = centred * lax.rsqrt(var + eps)
    gated = (normed * proj_ref[:, 0:feature].astype(jnp.float32)).astype(jnp.bfloat16)
    update = jnp.dot(gated, wout_ref[...], preferred_element_type=jnp.float32)
    out_ref[...] = (rows_ref[...].astype(jnp.float32) + update).astype(out_ref.dtype)

def tail(lengths, projected, cache, rows, wout, heads=8, eps=1e-6, group=2):
    members, hist, doubled = cache.shape
    slots, feature = rows.shape
    per = slots // members * group
    width = projected.shape[1]
    kern = functools.partial(tail_kernel, heads=heads, eps=eps)
    spec = pltpu.PrefetchScalarGridSpec(
        num_scalar_prefetch=1, grid=(members // group,),
        in_specs=[pl.BlockSpec((per, width), lambda b, n: (b, 0)),
                  pl.BlockSpec((group, hist, doubled), lambda b, n: (b, 0, 0)),
                  pl.BlockSpec((per, feature), lambda b, n: (b, 0)),
                  pl.BlockSpec((feature, feature), lambda b, n: (0, 0))],
        out_specs=pl.BlockSpec((per, feature), lambda b, n: (b, 0)),
        scratch_shapes=[pltpu.VMEM((per, feature), jnp.float32)])
    return pl.pallas_call(kern, grid_spec=spec, out_shape=jax.ShapeDtypeStruct((slots, feature), jnp.bfloat16),
        cost_estimate=pl.CostEstimate(flops=2*slots*feature*feature + 4*slots*hist*feature, transcendentals=slots*(hist*heads+heads), bytes_accessed=slots*width*2 + members*hist*doubled*2 + 2*slots*feature*2 + feature*feature*2))(lengths, projected, cache, rows, wout)


def ranks(targets, sources):
    count = targets.shape[0]
    one_hot = (targets[:, None] == jnp.arange(sources, dtype=jnp.int32)[None, :])
    rows = jnp.arange(count, dtype=jnp.int32)
    lower = (rows[None, :] < rows[:, None]).astype(jnp.bfloat16)
    earlier = jnp.dot(lower, one_hot.astype(jnp.bfloat16), preferred_element_type=jnp.float32)
    return jnp.sum(jnp.where(one_hot, earlier, 0.0), axis=1).astype(jnp.int32)


def block_plan(ints, half, n_half, per_pair, sources):
    picks, targets, places = ints[0], ints[1], ints[2]
    within = ranks(targets, sources)
    keep = (targets // n_half) == half
    position = jnp.where(keep, (targets % n_half) * per_pair + within, -1)
    spots = jnp.arange(n_half * per_pair, dtype=jnp.int32)
    hit = position[None, :] == spots[:, None]
    row = jnp.sum(jnp.where(hit, picks[None, :], 0), axis=1)
    slot = jnp.sum(jnp.where(hit, places[None, :] + 1, 0), axis=1) - 1
    return row.reshape(n_half, per_pair), slot.reshape(n_half, per_pair)


def select_rows(table, rows, slots):
    flat_rows = rows.reshape(-1)
    used = slots.reshape(-1) >= 0
    entries = jnp.arange(table.shape[0], dtype=jnp.int32)
    one_hot = ((flat_rows[:, None] == entries[None, :]) & used[:, None]).astype(table.dtype)
    picked = jnp.dot(one_hot, table, preferred_element_type=jnp.float32).astype(table.dtype)
    return picked.reshape(rows.shape + (table.shape[1],))


def place_rows(arrived, tags, slot_ids):
    rows = arrived.reshape(-1, arrived.shape[-1])
    one_hot = (slot_ids[:, None] == tags.reshape(-1)[None, :]).astype(rows.dtype)
    return jnp.dot(one_hot, rows, preferred_element_type=jnp.float32)


def shards(
    item_table,
    picked_items,
    destination,
    slot_index,
    history_cache,
    history_length,
    input_weight,
    output_weight,
):
    n_half = lax.axis_size("xy")
    sources = HALVES * n_half
    half = lax.axis_index("zh")
    item_rows = item_table[0, 0]
    ints = jnp.stack([picked_items[0, 0], destination[0, 0], slot_index[0, 0]])
    slot_count = ints.shape[1]
    feature = item_rows.shape[1]
    per_pair = 2 * slot_count // sources
    swap = [(0, 1), (1, 0)]
    table_span = item_rows.shape[0]
    coded = jnp.stack(
        [ints[0], ints[1], jnp.floor_divide(ints[2], RADIX), ints[2] % RADIX]
    ).astype(jnp.bfloat16)
    spare = jnp.zeros((CODE_ROWS - coded.shape[0], feature), jnp.bfloat16)
    bundle = jnp.concatenate([item_rows, coded, spare], axis=0)
    received = lax.ppermute(bundle, "zh", swap)
    other_rows = received[:table_span]
    codes = received[table_span : table_span + 4].astype(jnp.int32)
    other_ints = jnp.stack([codes[0], codes[1], codes[2] * RADIX + codes[3]])

    own_row, own_slot = block_plan(ints, half, n_half, per_pair, sources)
    far_row, far_slot = block_plan(other_ints, half, n_half, per_pair, sources)
    own_data = select_rows(item_rows, own_row, own_slot)
    far_data = select_rows(other_rows, far_row, far_slot)
    slots = jnp.concatenate([own_slot, far_slot], axis=1)
    capacity = 2 * per_pair
    own_arrived = lax.all_to_all(own_data, "xy", split_axis=0, concat_axis=0, tiled=True)
    slots, own_arrived = lax.optimization_barrier((slots, own_arrived))
    tags = lax.all_to_all(slots, "xy", split_axis=0, concat_axis=0, tiled=True)
    tags, far_data = lax.optimization_barrier((tags, far_data))
    far_arrived = lax.all_to_all(far_data, "xy", split_axis=0, concat_axis=0, tiled=True)
    slot_ids = jnp.arange(slot_count, dtype=jnp.int32)
    tags = tags.reshape(n_half, 2, per_pair)
    as_float = place_rows(own_arrived, tags[:, 0], slot_ids) + place_rows(
        far_arrived, tags[:, 1], slot_ids
    )
    arranged = as_float.astype(jnp.bfloat16)

    lengths = history_length[0]
    normed_in = layer_norm(as_float).astype(jnp.bfloat16)
    projected = jax.nn.silu(
        jnp.dot(normed_in, input_weight, preferred_element_type=jnp.float32)
    ).astype(jnp.bfloat16)
    cache = lax.all_gather(history_cache, "cand", axis=1, tiled=True)[0]
    mixed = tail(lengths, projected, cache, arranged, output_weight)
    return mixed[None, None]


def solution(mesh):
    n_req, n_cand = mesh.devices.shape
    devices = mesh.devices.reshape(HALVES, n_req // HALVES, n_cand)
    split = Mesh(devices, ("zh", "xy", "cand"))
    req = ("zh", "xy")
    in_specs = (
        P(req, "cand", None, None),
        P(req, "cand", None),
        P(req, "cand", None),
        P(req, "cand", None),
        P(req, "cand", None, None),
        P(req, None),
        P(),
        P(),
    )
    out_specs = P(req, "cand", None, None)
    return jax.shard_map(shards, mesh=split, in_specs=in_specs, out_specs=out_specs, check_vma=False)
```

```python
import math

import functools

import jax
import jax.numpy as jnp
from jax import lax
from jax.experimental import pallas as pl
from jax.experimental.pallas import tpu as pltpu
from jax.sharding import Mesh
from jax.sharding import PartitionSpec as P

HEADS = 8
HALVES = 2
RADIX = 32
CODE_ROWS = 16


epsilon = 1e-06


def layer_norm(values):
    average = jnp.mean(values, axis=-1, keepdims=True)
    centred = values - average
    variance = jnp.mean(centred * centred, axis=-1, keepdims=True)
    return centred * lax.rsqrt(variance + epsilon)


def silu(v):
    return v / (1.0 + jnp.exp(-v))

def tail_kernel(len_ref, proj_ref, cache_ref, rows_ref, wout_ref, out_ref, att_ref, *, heads, eps):
    step = pl.program_id(0)
    group, hist, doubled = cache_ref.shape
    per = rows_ref.shape[0] // group
    feature = rows_ref.shape[1]
    head_width = feature // heads
    scale = 1.0 / math.sqrt(head_width)
    for member in range(group):
        length = len_ref[step * group + member]
        inverse = 1.0 / (length.astype(jnp.float32) + 1.0)
        valid = lax.broadcasted_iota(jnp.int32, (1, hist), 1) < length
        rows = pl.ds(member * per, per)
        for h in range(heads):
            lo = h * head_width
            q = proj_ref[rows, 2 * feature + lo : 2 * feature + lo + head_width]
            k = cache_ref[member, :, lo : lo + head_width]
            v = cache_ref[member, :, feature + lo : feature + lo + head_width]
            s = lax.dot_general(q, k, (((1,), (1,)), ((), ())), preferred_element_type=jnp.float32) * scale
            w = jnp.where(valid, silu(s) * inverse, 0.0).astype(jnp.bfloat16)
            found = jnp.dot(w, v, preferred_element_type=jnp.float32)
            own_k = proj_ref[rows, 3 * feature + lo : 3 * feature + lo + head_width].astype(jnp.float32)
            own_v = proj_ref[rows, feature + lo : feature + lo + head_width].astype(jnp.float32)
            own_s = jnp.sum(q.astype(jnp.float32) * own_k, axis=-1, keepdims=True) * scale
            att_ref[rows, lo : lo + head_width] = found + (silu(own_s) * inverse) * own_v
    att = att_ref[...]
    mean = jnp.mean(att, axis=-1, keepdims=True)
    centred = att - mean
    var = jnp.mean(centred * centred, axis=-1, keepdims=True)
    normed = centred * lax.rsqrt(var + eps)
    gated = (normed * proj_ref[:, 0:feature].astype(jnp.float32)).astype(jnp.bfloat16)
    update = jnp.dot(gated, wout_ref[...], preferred_element_type=jnp.float32)
    out_ref[...] = (rows_ref[...].astype(jnp.float32) + update).astype(out_ref.dtype)

def tail(lengths, projected, cache, rows, wout, heads=8, eps=1e-6, group=2):
    members, hist, doubled = cache.shape
    slots, feature = rows.shape
    per = slots // members * group
    width = projected.shape[1]
    kern = functools.partial(tail_kernel, heads=heads, eps=eps)
    spec = pltpu.PrefetchScalarGridSpec(
        num_scalar_prefetch=1, grid=(members // group,),
        in_specs=[pl.BlockSpec((per, width), lambda b, n: (b, 0)),
                  pl.BlockSpec((group, hist, doubled), lambda b, n: (b, 0, 0)),
                  pl.BlockSpec((per, feature), lambda b, n: (b, 0)),
                  pl.BlockSpec((feature, feature), lambda b, n: (0, 0))],
        out_specs=pl.BlockSpec((per, feature), lambda b, n: (b, 0)),
        scratch_shapes=[pltpu.VMEM((per, feature), jnp.float32)])
    return pl.pallas_call(kern, grid_spec=spec, out_shape=jax.ShapeDtypeStruct((slots, feature), jnp.bfloat16),
        cost_estimate=pl.CostEstimate(flops=2*slots*feature*feature + 4*slots*hist*feature, transcendentals=slots*(hist*heads+heads), bytes_accessed=slots*width*2 + members*hist*doubled*2 + 2*slots*feature*2 + feature*feature*2))(lengths, projected, cache, rows, wout)


def ranks(targets, sources):
    count = targets.shape[0]
    one_hot = (targets[:, None] == jnp.arange(sources, dtype=jnp.int32)[None, :])
    rows = jnp.arange(count, dtype=jnp.int32)
    lower = (rows[None, :] < rows[:, None]).astype(jnp.bfloat16)
    earlier = jnp.dot(lower, one_hot.astype(jnp.bfloat16), preferred_element_type=jnp.float32)
    return jnp.sum(jnp.where(one_hot, earlier, 0.0), axis=1).astype(jnp.int32)


def block_plan(ints, half, n_half, per_pair, sources):
    picks, targets, places = ints[0], ints[1], ints[2]
    within = ranks(targets, sources)
    keep = (targets // n_half) == half
    position = jnp.where(keep, (targets % n_half) * per_pair + within, -1)
    spots = jnp.arange(n_half * per_pair, dtype=jnp.int32)
    hit = position[None, :] == spots[:, None]
    row = jnp.sum(jnp.where(hit, picks[None, :], 0), axis=1)
    slot = jnp.sum(jnp.where(hit, places[None, :] + 1, 0), axis=1) - 1
    return row.reshape(n_half, per_pair), slot.reshape(n_half, per_pair)


def select_rows(table, rows, slots):
    flat_rows = rows.reshape(-1)
    used = slots.reshape(-1) >= 0
    entries = jnp.arange(table.shape[0], dtype=jnp.int32)
    one_hot = ((flat_rows[:, None] == entries[None, :]) & used[:, None]).astype(table.dtype)
    picked = jnp.dot(one_hot, table, preferred_element_type=jnp.float32).astype(table.dtype)
    return picked.reshape(rows.shape + (table.shape[1],))


TAG_LANES = 128


def with_tags(data, *slot_lists):
    lane = lax.broadcasted_iota(jnp.int32, data.shape[:-1] + (TAG_LANES,), 2)
    tags = jnp.zeros(lane.shape, jnp.int32)
    for n, slots in enumerate(slot_lists):
        high = jnp.floor_divide(slots, RADIX)
        low = slots - high * RADIX
        tags = jnp.where(lane == 2 * n, high[..., None], tags)
        tags = jnp.where(lane == 2 * n + 1, low[..., None], tags)
    return jnp.concatenate([data, tags.astype(data.dtype)], axis=-1)


def place_rows(arrived, tags, slot_ids):
    rows = arrived.reshape(-1, arrived.shape[-1])
    one_hot = (slot_ids[:, None] == tags.reshape(-1)[None, :]).astype(rows.dtype)
    return jnp.dot(one_hot, rows, preferred_element_type=jnp.float32)


def shards(
    item_table,
    picked_items,
    destination,
    slot_index,
    history_cache,
    history_length,
    input_weight,
    output_weight,
):
    n_half = lax.axis_size("xy")
    sources = HALVES * n_half
    half = lax.axis_index("zh")
    item_rows = item_table[0, 0]
    ints = jnp.stack([picked_items[0, 0], destination[0, 0], slot_index[0, 0]])
    slot_count = ints.shape[1]
    feature = item_rows.shape[1]
    per_pair = 2 * slot_count // sources
    swap = [(0, 1), (1, 0)]
    table_span = item_rows.shape[0]
    coded = jnp.stack(
        [ints[0], ints[1], jnp.floor_divide(ints[2], RADIX), ints[2] % RADIX]
    ).astype(jnp.bfloat16)
    spare = jnp.zeros((CODE_ROWS - coded.shape[0], feature), jnp.bfloat16)
    bundle = jnp.concatenate([item_rows, coded, spare], axis=0)
    received = lax.ppermute(bundle, "zh", swap)
    other_rows = received[:table_span]
    codes = received[table_span : table_span + 4].astype(jnp.int32)
    other_ints = jnp.stack([codes[0], codes[1], codes[2] * RADIX + codes[3]])

    own_row, own_slot = block_plan(ints, half, n_half, per_pair, sources)
    far_row, far_slot = block_plan(other_ints, half, n_half, per_pair, sources)
    own_data = select_rows(item_rows, own_row, own_slot)
    far_data = select_rows(other_rows, far_row, far_slot)
    own_arrived = lax.all_to_all(own_data, "xy", split_axis=0, concat_axis=0, tiled=True)
    payload, own_arrived = lax.optimization_barrier(
        (with_tags(far_data, far_slot, own_slot), own_arrived)
    )
    far_arrived = lax.all_to_all(payload, "xy", split_axis=0, concat_axis=0, tiled=True)
    far_rows = far_arrived[..., :feature]
    codes = far_arrived[..., feature : feature + 4].astype(jnp.int32)
    far_tags = codes[..., 0] * RADIX + codes[..., 1]
    own_tags = codes[..., 2] * RADIX + codes[..., 3]
    slot_ids = jnp.arange(slot_count, dtype=jnp.int32)
    as_float = place_rows(own_arrived, own_tags, slot_ids) + place_rows(
        far_rows, far_tags, slot_ids
    )
    arranged = as_float.astype(jnp.bfloat16)

    lengths = history_length[0]
    normed_in = layer_norm(as_float).astype(jnp.bfloat16)
    projected = jax.nn.silu(
        jnp.dot(normed_in, input_weight, preferred_element_type=jnp.float32)
    ).astype(jnp.bfloat16)
    cache = lax.all_gather(history_cache, "cand", axis=1, tiled=True)[0]
    mixed = tail(lengths, projected, cache, arranged, output_weight)
    return mixed[None, None]


def solution(mesh):
    n_req, n_cand = mesh.devices.shape
    devices = mesh.devices.reshape(HALVES, n_req // HALVES, n_cand)
    split = Mesh(devices, ("zh", "xy", "cand"))
    req = ("zh", "xy")
    in_specs = (
        P(req, "cand", None, None),
        P(req, "cand", None),
        P(req, "cand", None),
        P(req, "cand", None),
        P(req, "cand", None, None),
        P(req, None),
        P(),
        P(),
    )
    out_specs = P(req, "cand", None, None)
    return jax.shard_map(shards, mesh=split, in_specs=in_specs, out_specs=out_specs, check_vma=False)
```

```python
import math

import functools

import jax
import jax.numpy as jnp
from jax import lax
from jax.experimental import pallas as pl
from jax.experimental.pallas import tpu as pltpu
from jax.sharding import Mesh
from jax.sharding import PartitionSpec as P

HEADS = 8
HALVES = 2


epsilon = 1e-06


def layer_norm(values):
    average = jnp.mean(values, axis=-1, keepdims=True)
    centred = values - average
    variance = jnp.mean(centred * centred, axis=-1, keepdims=True)
    return centred * lax.rsqrt(variance + epsilon)


def silu(v):
    return v * (0.5 + 0.5 * jnp.tanh(0.5 * v))

def tail_kernel(len_ref, proj_ref, cache_ref, rows_ref, wout_ref, out_ref, att_ref, *, heads, eps):
    step = pl.program_id(0)
    group, hist, doubled = cache_ref.shape
    per = rows_ref.shape[0] // group
    feature = rows_ref.shape[1]
    head_width = feature // heads
    scale = 1.0 / math.sqrt(head_width)
    for member in range(group):
        length = len_ref[step * group + member]
        inverse = 1.0 / (length.astype(jnp.float32) + 1.0)
        valid = lax.broadcasted_iota(jnp.int32, (1, hist), 1) < length
        rows = pl.ds(member * per, per)
        for h in range(heads):
            lo = h * head_width
            q = proj_ref[rows, 2 * feature + lo : 2 * feature + lo + head_width]
            k = cache_ref[member, :, lo : lo + head_width]
            v = cache_ref[member, :, feature + lo : feature + lo + head_width]
            s = lax.dot_general(q, k, (((1,), (1,)), ((), ())), preferred_element_type=jnp.float32) * scale
            w = jnp.where(valid, silu(s) * inverse, 0.0).astype(jnp.bfloat16)
            found = jnp.dot(w, v, preferred_element_type=jnp.float32)
            own_k = proj_ref[rows, 3 * feature + lo : 3 * feature + lo + head_width].astype(jnp.float32)
            own_v = proj_ref[rows, feature + lo : feature + lo + head_width].astype(jnp.float32)
            own_s = jnp.sum(q.astype(jnp.float32) * own_k, axis=-1, keepdims=True) * scale
            att_ref[rows, lo : lo + head_width] = found + (silu(own_s) * inverse) * own_v
    att = att_ref[...]
    mean = jnp.mean(att, axis=-1, keepdims=True)
    centred = att - mean
    var = jnp.mean(centred * centred, axis=-1, keepdims=True)
    normed = centred * lax.rsqrt(var + eps)
    gated = (normed * proj_ref[:, 0:feature].astype(jnp.float32)).astype(jnp.bfloat16)
    update = jnp.dot(gated, wout_ref[...], preferred_element_type=jnp.float32)
    out_ref[...] = (rows_ref[...].astype(jnp.float32) + update).astype(out_ref.dtype)

def tail(lengths, projected, cache, rows, wout, heads=8, eps=1e-6, group=2):
    members, hist, doubled = cache.shape
    slots, feature = rows.shape
    per = slots // members * group
    width = projected.shape[1]
    kern = functools.partial(tail_kernel, heads=heads, eps=eps)
    spec = pltpu.PrefetchScalarGridSpec(
        num_scalar_prefetch=1, grid=(members // group,),
        in_specs=[pl.BlockSpec((per, width), lambda b, n: (b, 0)),
                  pl.BlockSpec((group, hist, doubled), lambda b, n: (b, 0, 0)),
                  pl.BlockSpec((per, feature), lambda b, n: (b, 0)),
                  pl.BlockSpec((feature, feature), lambda b, n: (0, 0))],
        out_specs=pl.BlockSpec((per, feature), lambda b, n: (b, 0)),
        scratch_shapes=[pltpu.VMEM((per, feature), jnp.float32)])
    params = pltpu.CompilerParams()
    return pl.pallas_call(kern, grid_spec=spec, out_shape=jax.ShapeDtypeStruct((slots, feature), jnp.bfloat16),
        compiler_params=params,
        cost_estimate=pl.CostEstimate(flops=2*slots*feature*feature + 4*slots*hist*feature, transcendentals=slots*(hist*heads+heads), bytes_accessed=slots*width*2 + members*hist*doubled*2 + 2*slots*feature*2 + feature*feature*2))(lengths, projected, cache, rows, wout)


def ranks(targets, sources):
    count = targets.shape[0]
    one_hot = (targets[:, None] == jnp.arange(sources, dtype=jnp.int32)[None, :])
    rows = jnp.arange(count, dtype=jnp.int32)
    lower = (rows[None, :] < rows[:, None]).astype(jnp.bfloat16)
    earlier = jnp.dot(lower, one_hot.astype(jnp.bfloat16), preferred_element_type=jnp.float32)
    return jnp.sum(jnp.where(one_hot, earlier, 0.0), axis=1).astype(jnp.int32)


def block_plan(ints, half, n_half, per_pair, sources):
    picks, targets, places = ints[0], ints[1], ints[2]
    within = ranks(targets, sources)
    keep = (targets // n_half) == half
    position = jnp.where(keep, (targets % n_half) * per_pair + within, -1)
    spots = jnp.arange(n_half * per_pair, dtype=jnp.int32)
    hit = position[None, :] == spots[:, None]
    row = jnp.sum(jnp.where(hit, picks[None, :], 0), axis=1)
    slot = jnp.sum(jnp.where(hit, places[None, :] + 1, 0), axis=1) - 1
    return row.reshape(n_half, per_pair), slot.reshape(n_half, per_pair)


def select_rows(table, rows, slots):
    flat_rows = rows.reshape(-1)
    used = slots.reshape(-1) >= 0
    entries = jnp.arange(table.shape[0], dtype=jnp.int32)
    one_hot = ((flat_rows[:, None] == entries[None, :]) & used[:, None]).astype(table.dtype)
    picked = jnp.dot(one_hot, table, preferred_element_type=jnp.float32).astype(table.dtype)
    return picked.reshape(rows.shape + (table.shape[1],))


def place_rows(arrived, tags, slot_ids):
    rows = arrived.reshape(-1, arrived.shape[-1])
    one_hot = (slot_ids[:, None] == tags.reshape(-1)[None, :]).astype(rows.dtype)
    return jnp.dot(one_hot, rows, preferred_element_type=jnp.float32)


def shards(
    item_table,
    picked_items,
    destination,
    slot_index,
    history_cache,
    history_length,
    input_weight,
    output_weight,
):
    n_half = lax.axis_size("xy")
    sources = HALVES * n_half
    half = lax.axis_index("zh")
    item_rows = item_table[0, 0]
    ints = jnp.stack([picked_items[0, 0], destination[0, 0], slot_index[0, 0]])
    slot_count = ints.shape[1]
    feature = item_rows.shape[1]
    per_pair = 2 * slot_count // sources
    swap = [(0, 1), (1, 0)]
    other_rows = lax.ppermute(item_rows, "zh", swap)
    other_ints = lax.ppermute(ints, "zh", swap)

    own_row, own_slot = block_plan(ints, half, n_half, per_pair, sources)
    far_row, far_slot = block_plan(other_ints, half, n_half, per_pair, sources)
    own_data = select_rows(item_rows, own_row, own_slot)
    far_data = select_rows(other_rows, far_row, far_slot)
    slots = jnp.concatenate([own_slot, far_slot], axis=1)
    capacity = 2 * per_pair
    every_slot = lax.all_gather(slots, "xy", axis=0, tiled=False)
    tags = lax.dynamic_index_in_dim(every_slot, lax.axis_index("xy"), axis=1, keepdims=False)
    tags = tags.reshape(-1)
    own_arrived = lax.all_to_all(own_data, "xy", split_axis=0, concat_axis=0, tiled=True)
    tags, far_data = lax.optimization_barrier((tags, far_data))
    far_arrived = lax.all_to_all(far_data, "xy", split_axis=0, concat_axis=0, tiled=True)
    slot_ids = jnp.arange(slot_count, dtype=jnp.int32)
    tags = tags.reshape(n_half, 2, per_pair)
    as_float = place_rows(own_arrived, tags[:, 0], slot_ids) + place_rows(
        far_arrived, tags[:, 1], slot_ids
    )
    arranged = as_float.astype(jnp.bfloat16)

    lengths = history_length[0]
    normed_in = layer_norm(as_float).astype(jnp.bfloat16)
    projected = jax.nn.silu(
        jnp.dot(normed_in, input_weight, preferred_element_type=jnp.float32)
    ).astype(jnp.bfloat16)
    cache = lax.all_gather(history_cache, "cand", axis=1, tiled=True)[0]
    mixed = tail(lengths, projected, cache, arranged, output_weight)
    return mixed[None, None]


def solution(mesh):
    n_req, n_cand = mesh.devices.shape
    devices = mesh.devices.reshape(HALVES, n_req // HALVES, n_cand)
    split = Mesh(devices, ("zh", "xy", "cand"))
    req = ("zh", "xy")
    in_specs = (
        P(req, "cand", None, None),
        P(req, "cand", None),
        P(req, "cand", None),
        P(req, "cand", None),
        P(req, "cand", None, None),
        P(req, None),
        P(),
        P(),
    )
    out_specs = P(req, "cand", None, None)
    return jax.shard_map(shards, mesh=split, in_specs=in_specs, out_specs=out_specs, check_vma=False)
```

```python
import math

import functools

import jax
import jax.numpy as jnp
from jax import lax
from jax.experimental import pallas as pl
from jax.experimental.pallas import tpu as pltpu
from jax.sharding import Mesh
from jax.sharding import PartitionSpec as P

HEADS = 8
HALVES = 2


epsilon = 1e-06


def layer_norm(values):
    average = jnp.mean(values, axis=-1, keepdims=True)
    centred = values - average
    variance = jnp.mean(centred * centred, axis=-1, keepdims=True)
    return centred * lax.rsqrt(variance + epsilon)


def silu(v):
    return v * (0.5 + 0.5 * jnp.tanh(0.5 * v))

def tail_kernel(len_ref, proj_ref, cache_ref, rows_ref, wout_ref, out_ref, att_ref, *, heads, eps):
    step = pl.program_id(0)
    group, hist, doubled = cache_ref.shape
    per = rows_ref.shape[0] // group
    feature = rows_ref.shape[1]
    head_width = feature // heads
    scale = 1.0 / math.sqrt(head_width)
    for member in range(group):
        length = len_ref[step * group + member]
        inverse = 1.0 / (length.astype(jnp.float32) + 1.0)
        valid = lax.broadcasted_iota(jnp.int32, (1, hist), 1) < length
        rows = pl.ds(member * per, per)
        for h in range(heads):
            lo = h * head_width
            q = proj_ref[rows, 2 * feature + lo : 2 * feature + lo + head_width]
            k = cache_ref[member, :, lo : lo + head_width]
            v = cache_ref[member, :, feature + lo : feature + lo + head_width]
            s = lax.dot_general(q, k, (((1,), (1,)), ((), ())), preferred_element_type=jnp.float32) * scale
            w = jnp.where(valid, silu(s) * inverse, 0.0).astype(jnp.bfloat16)
            found = jnp.dot(w, v, preferred_element_type=jnp.float32)
            own_k = proj_ref[rows, 3 * feature + lo : 3 * feature + lo + head_width].astype(jnp.float32)
            own_v = proj_ref[rows, feature + lo : feature + lo + head_width].astype(jnp.float32)
            own_s = jnp.sum(q.astype(jnp.float32) * own_k, axis=-1, keepdims=True) * scale
            att_ref[rows, lo : lo + head_width] = found + (silu(own_s) * inverse) * own_v
    att = att_ref[...]
    mean = jnp.mean(att, axis=-1, keepdims=True)
    centred = att - mean
    var = jnp.mean(centred * centred, axis=-1, keepdims=True)
    normed = centred * lax.rsqrt(var + eps)
    gated = (normed * proj_ref[:, 0:feature].astype(jnp.float32)).astype(jnp.bfloat16)
    update = jnp.dot(gated, wout_ref[...], preferred_element_type=jnp.float32)
    out_ref[...] = (rows_ref[...].astype(jnp.float32) + update).astype(out_ref.dtype)

def tail(lengths, projected, cache, rows, wout, heads=8, eps=1e-6, group=4):
    members, hist, doubled = cache.shape
    slots, feature = rows.shape
    per = slots // members * group
    width = projected.shape[1]
    kern = functools.partial(tail_kernel, heads=heads, eps=eps)
    spec = pltpu.PrefetchScalarGridSpec(
        num_scalar_prefetch=1, grid=(members // group,),
        in_specs=[pl.BlockSpec((per, width), lambda b, n: (b, 0)),
                  pl.BlockSpec((group, hist, doubled), lambda b, n: (b, 0, 0)),
                  pl.BlockSpec((per, feature), lambda b, n: (b, 0)),
                  pl.BlockSpec((feature, feature), lambda b, n: (0, 0))],
        out_specs=pl.BlockSpec((per, feature), lambda b, n: (b, 0)),
        scratch_shapes=[pltpu.VMEM((per, feature), jnp.float32)])
    params = pltpu.CompilerParams()
    return pl.pallas_call(kern, grid_spec=spec, out_shape=jax.ShapeDtypeStruct((slots, feature), jnp.bfloat16),
        compiler_params=params,
        cost_estimate=pl.CostEstimate(flops=2*slots*feature*feature + 4*slots*hist*feature, transcendentals=slots*(hist*heads+heads), bytes_accessed=slots*width*2 + members*hist*doubled*2 + 2*slots*feature*2 + feature*feature*2))(lengths, projected, cache, rows, wout)


def ranks(targets, sources):
    count = targets.shape[0]
    one_hot = (targets[:, None] == jnp.arange(sources, dtype=jnp.int32)[None, :])
    rows = jnp.arange(count, dtype=jnp.int32)
    lower = (rows[None, :] < rows[:, None]).astype(jnp.bfloat16)
    earlier = jnp.dot(lower, one_hot.astype(jnp.bfloat16), preferred_element_type=jnp.float32)
    return jnp.sum(jnp.where(one_hot, earlier, 0.0), axis=1).astype(jnp.int32)


def block_plan(ints, half, n_half, per_pair, sources):
    picks, targets, places = ints[0], ints[1], ints[2]
    within = ranks(targets, sources)
    keep = (targets // n_half) == half
    position = jnp.where(keep, (targets % n_half) * per_pair + within, -1)
    spots = jnp.arange(n_half * per_pair, dtype=jnp.int32)
    hit = position[None, :] == spots[:, None]
    row = jnp.sum(jnp.where(hit, picks[None, :], 0), axis=1)
    slot = jnp.sum(jnp.where(hit, places[None, :] + 1, 0), axis=1) - 1
    return row.reshape(n_half, per_pair), slot.reshape(n_half, per_pair)


def select_rows(table, rows, slots):
    flat_rows = rows.reshape(-1)
    used = slots.reshape(-1) >= 0
    entries = jnp.arange(table.shape[0], dtype=jnp.int32)
    one_hot = ((flat_rows[:, None] == entries[None, :]) & used[:, None]).astype(table.dtype)
    picked = jnp.dot(one_hot, table, preferred_element_type=jnp.float32).astype(table.dtype)
    return picked.reshape(rows.shape + (table.shape[1],))


def place_rows(arrived, tags, slot_ids):
    rows = arrived.reshape(-1, arrived.shape[-1])
    one_hot = (slot_ids[:, None] == tags.reshape(-1)[None, :]).astype(rows.dtype)
    return jnp.dot(one_hot, rows, preferred_element_type=jnp.float32)


def shards(
    item_table,
    picked_items,
    destination,
    slot_index,
    history_cache,
    history_length,
    input_weight,
    output_weight,
):
    n_half = lax.axis_size("xy")
    sources = HALVES * n_half
    half = lax.axis_index("zh")
    item_rows = item_table[0, 0]
    ints = jnp.stack([picked_items[0, 0], destination[0, 0], slot_index[0, 0]])
    slot_count = ints.shape[1]
    feature = item_rows.shape[1]
    per_pair = 2 * slot_count // sources
    swap = [(0, 1), (1, 0)]
    other_rows = lax.ppermute(item_rows, "zh", swap)
    other_ints = lax.ppermute(ints, "zh", swap)

    own_row, own_slot = block_plan(ints, half, n_half, per_pair, sources)
    far_row, far_slot = block_plan(other_ints, half, n_half, per_pair, sources)
    own_data = select_rows(item_rows, own_row, own_slot)
    far_data = select_rows(other_rows, far_row, far_slot)
    slots = jnp.concatenate([own_slot, far_slot], axis=1)
    capacity = 2 * per_pair
    every_slot = lax.all_gather(slots, "xy", axis=0, tiled=False)
    tags = lax.dynamic_index_in_dim(every_slot, lax.axis_index("xy"), axis=1, keepdims=False)
    tags = tags.reshape(-1)
    own_arrived = lax.all_to_all(own_data, "xy", split_axis=0, concat_axis=0, tiled=True)
    tags, far_data = lax.optimization_barrier((tags, far_data))
    far_arrived = lax.all_to_all(far_data, "xy", split_axis=0, concat_axis=0, tiled=True)
    slot_ids = jnp.arange(slot_count, dtype=jnp.int32)
    tags = tags.reshape(n_half, 2, per_pair)
    as_float = place_rows(own_arrived, tags[:, 0], slot_ids) + place_rows(
        far_arrived, tags[:, 1], slot_ids
    )
    arranged = as_float.astype(jnp.bfloat16)

    lengths = history_length[0]
    normed_in = layer_norm(as_float).astype(jnp.bfloat16)
    projected = jax.nn.silu(
        jnp.dot(normed_in, input_weight, preferred_element_type=jnp.float32)
    ).astype(jnp.bfloat16)
    cache = lax.all_gather(history_cache, "cand", axis=1, tiled=True)[0]
    mixed = tail(lengths, projected, cache, arranged, output_weight)
    return mixed[None, None]


def solution(mesh):
    n_req, n_cand = mesh.devices.shape
    devices = mesh.devices.reshape(HALVES, n_req // HALVES, n_cand)
    split = Mesh(devices, ("zh", "xy", "cand"))
    req = ("zh", "xy")
    in_specs = (
        P(req, "cand", None, None),
        P(req, "cand", None),
        P(req, "cand", None),
        P(req, "cand", None),
        P(req, "cand", None, None),
        P(req, None),
        P(),
        P(),
    )
    out_specs = P(req, "cand", None, None)
    return jax.shard_map(shards, mesh=split, in_specs=in_specs, out_specs=out_specs, check_vma=False)
```
